32 devices in a mesh: grp: 8 (over z, x), rep: 4 (over y, core).
Axes of the slice: x: 2, y: 2, z: 4, core: 2. Of those that a mesh axis runs over, the one named last changes fastest.
Arguments:
- three_center: bfloat16 [4, 64, 32, 6, 4096], P('rep', 'grp'), may hold values from -2 to 2
- metric: bfloat16 [4, 64, 64], P('rep'), may hold values from -0.75 to 0.75
- occupied: bfloat16 [2048, 48], replicated, may hold values from -0.3125 to 0.3125
- nu_list: int32 [32, 6], replicated, may hold values from 0 to 31, as said below
- nu_count: int32 [32], replicated, may hold values from 1 to 6
- block_size: int32 [32], replicated, may hold values from 32 to 64
Outputs:
- exchange_matrix: float32 [2048, 2048], P('rep', 'grp')
The draws below stay inside these ranges and needn't reach their ends.
Inputs may be any that keep to these rules, and one draw needn't show every extreme that they name: `nu_list`: entry 0 of row m is m itself; the other entries of a row are distinct blocks other than m.
All inputs are finite; a program needn't handle non-finite values.
Results may differ from the reference program's by a relative error of at most 0.0024.
Values may be sent and summed in bfloat16 or wider, within the bound.
No kernel may reach another device: no remote copies, remote signals or barrier semaphores. Data moves between devices by JAX's collectives and lax.ppermute only.
A program may use at most 192 MiB of HBM per device.

```python
import jax
import jax.numpy as jnp
from jax import lax

NB = 64
KNU = 6
NOCC = 48
NMU = 32
NBAS = 2048
NAUX_GRP = 64
N_REP = 4


def draw_nu_list(key, part):
    rows = jnp.arange(NMU, dtype=jnp.int32)
    keys = jax.random.split(key, NMU)
    offsets = jax.vmap(lambda one: jax.random.permutation(one, NMU - 1)[:KNU - 1])(keys)
    offsets = offsets.astype(jnp.int32) + 1
    others = (rows[:, None] + offsets) % NMU
    return jnp.concatenate([rows[:, None], others], axis=1).astype(jnp.int32)


def draw_nu_count(key, part):
    counts = jax.random.randint(key, (NMU,), 1, KNU + 1, dtype=jnp.int32)
    return counts.at[0].set(KNU).at[1].set(1)


def draw_block_size(key, part):
    sizes = jax.random.randint(key, (NMU,), NB // 2, NB + 1, dtype=jnp.int32)
    return sizes.at[0].set(NB).at[1].set(NB // 2)


def levels(rng, extent, cuts, least, high):
    gain = 1.0
    for axis_at, shards_of in cuts:
        heights = jax.random.uniform(jax.random.fold_in(jax.random.fold_in(rng, 6), axis_at), (shards_of,), jnp.float32, least / len(cuts), high / len(cuts))
        gain = gain * jnp.repeat(jnp.exp(heights), extent[axis_at] // shards_of).reshape((-1,) + (1,) * (len(extent) - 1 - axis_at))
    return gain


def gaussian(stream_key, dims, width, reach, cuts=(), held_as=jnp.bfloat16):
    entries = width * jax.random.normal(stream_key, dims, jnp.float32)
    if cuts:
        entries = entries * levels(stream_key, dims, cuts, -0.22, 0.18)
    return jnp.clip(entries, -reach, reach).astype(held_as)


def setup_inputs(seed: int = 0) -> dict:
    key_list = jax.random.split(jax.random.key(seed), 7)
    three_center = gaussian(key_list[0], (N_REP, NAUX_GRP, NMU, KNU, NB * NB), 0.15, 2.0, ((0, 4), (1, 8)))
    metric = gaussian(key_list[1], (N_REP, NAUX_GRP, NAUX_GRP), NAUX_GRP ** -0.5, 0.75, ((0, 4),))
    occupied = gaussian(key_list[2], (NBAS, NOCC), (KNU * NB) ** -0.5, 0.3125)
    nu_list = draw_nu_list(jax.random.fold_in(key_list[6], 71), 0)
    nu_count = draw_nu_count(jax.random.fold_in(key_list[6], 71), 0)
    block_size = draw_block_size(jax.random.fold_in(key_list[6], 71), 0)
    return dict(three_center=three_center, metric=metric, occupied=occupied, nu_list=nu_list, nu_count=nu_count, block_size=block_size)


def reference(three_center, metric, occupied, nu_list, nu_count, block_size):
    lanes = jnp.arange(NB, dtype=jnp.int32)
    row_live = lanes[None, :] < block_size[:, None]
    col_live = lanes[None, None, :] < block_size[nu_list][:, :, None]
    slot_live = jnp.arange(KNU, dtype=jnp.int32)[None, :] < nu_count[:, None]
    mask = row_live[:, None, :, None] & col_live[:, :, None, :] & slot_live[:, :, None, None]
    picked = occupied.reshape(NMU, NB, NOCC)[nu_list].astype(jnp.float32)

    def one_batch(pair):
        tensor, factor = pair
        blocks = tensor.astype(jnp.float32).reshape(NAUX_GRP, NMU, KNU, NB, NB)
        masked = jnp.where(mask[None], blocks, jnp.float32(0.0))
        half = jnp.einsum("qmkab,mkbi->qmai", masked, picked).astype(jnp.bfloat16)
        half = lax.optimization_barrier(half)
        orbital = jnp.einsum("pq,qmai->mapi", factor.astype(jnp.float32), half.astype(jnp.float32)).astype(jnp.bfloat16)
        return orbital.reshape(NBAS, NAUX_GRP * NOCC)

    orbitals = lax.map(one_batch, (three_center, metric))
    columns = jnp.transpose(orbitals, (1, 0, 2)).reshape(NBAS, N_REP * NAUX_GRP * NOCC)
    return jnp.dot(columns, columns.T, preferred_element_type=jnp.float32)
```

```python
import jax
import jax.numpy as jnp
from jax import lax
from jax.sharding import PartitionSpec as P

NB = 64
N_CHUNKS = 4


def body(three_center, metric, occupied, nu_list, nu_count, block_size):
    n_mu, knu = nu_list.shape
    n_occ = occupied.shape[1]
    aux_dev = three_center.shape[1]
    occ_c = n_occ // N_CHUNKS
    lanes = jnp.arange(NB, dtype=jnp.int32)
    row_live = lanes[None, :] < block_size[:, None]
    col_live = lanes[None, None, :] < block_size[nu_list][:, :, None]
    slot_live = jnp.arange(knu, dtype=jnp.int32)[None, :] < nu_count[:, None]
    mask = row_live[:, None, :, None] & col_live[:, :, None, :] & slot_live[:, :, None, None]
    blocks = three_center[0].reshape(aux_dev, n_mu, knu, NB, NB)
    masked = jnp.where(mask[None], blocks, jnp.zeros((), jnp.bfloat16))
    picked = occupied.reshape(n_mu, NB, N_CHUNKS, occ_c)[nu_list]
    half = jnp.einsum(
        "qmkab,mkbci->cqmai", masked, picked, preferred_element_type=jnp.float32
    ).astype(jnp.bfloat16)
    half = half.reshape(N_CHUNKS, aux_dev, n_mu, NB * occ_c)
    n_grp = lax.axis_size("grp")
    rows = n_mu * NB // n_grp
    start = lax.axis_index("grp") * rows
    term = None
    for c in range(N_CHUNKS):
        gathered = lax.all_gather(half[c], "grp", axis=0, tiled=True)
        n_aux = gathered.shape[0]
        gathered = gathered.reshape(n_aux, n_mu, NB, occ_c)
        orbital = jnp.einsum(
            "pq,qmai->mapi", metric[0], gathered, preferred_element_type=jnp.float32
        ).astype(jnp.bfloat16)
        orbital = orbital.reshape(n_mu * NB, n_aux * occ_c)
        mine = lax.dynamic_slice_in_dim(orbital, start, rows, axis=0)
        part = jnp.dot(orbital, mine.T, preferred_element_type=jnp.float32)
        term = part if term is None else term + part
    return lax.psum_scatter(term, "rep", scatter_dimension=0, tiled=True)


def solution(mesh):
    return jax.shard_map(
        body,
        mesh=mesh,
        in_specs=(P("rep", "grp", None, None, None), P("rep", None, None), P(), P(), P(), P()),
        out_specs=P("rep", "grp"),
        check_vma=False,
    )
```

```python
import jax
import jax.numpy as jnp
import numpy as np
from jax import lax
from jax.sharding import PartitionSpec as P

NB = 64


def snake(a_size, b_size):
    if a_size % 2:
        return [(a, b) for b, a in snake(b_size, a_size)]
    if b_size == 1:
        return [(a, 0) for a in range(a_size)]
    path = []
    for a in range(a_size):
        cols = range(b_size) if a == 0 else (range(1, b_size) if a % 2 == 0 else range(b_size - 1, 0, -1))
        path += [(a, b) for b in cols]
    path += [(a, 0) for a in range(a_size - 1, 0, -1)]
    return path


def ring_order(mesh):
    n = mesh.shape["grp"]
    try:
        devs = np.asarray(mesh.devices).reshape(n, -1)[:, 0]
        coords = [tuple(d.coords) for d in devs]
    except (AttributeError, TypeError):
        return list(range(n))
    varying = [i for i in range(len(coords[0])) if len({c[i] for c in coords}) > 1]
    if len(varying) == 1:
        key = sorted(range(n), key=lambda g: coords[g][varying[0]])
        return key
    if len(varying) != 2:
        return list(range(n))
    i, j = varying
    avals = sorted({c[i] for c in coords})
    bvals = sorted({c[j] for c in coords})
    where = {(avals.index(c[i]), bvals.index(c[j])): g for g, c in enumerate(coords)}
    if len(where) != n:
        return list(range(n))
    return [where[p] for p in snake(len(avals), len(bvals))]


def make_body(ring):
    n = len(ring)
    pos_of = np.zeros(n, np.int32)
    for p, g in enumerate(ring):
        pos_of[g] = p
    ring_arr = np.asarray(ring, np.int32)
    fwd = [(ring[p], ring[(p + 1) % n]) for p in range(n)]
    bwd = [(ring[p], ring[(p - 1) % n]) for p in range(n)]

    def body(three_center, metric, occupied, nu_list, nu_count, block_size):
        n_mu, knu = nu_list.shape
        n_occ = occupied.shape[1]
        aux_dev = three_center.shape[1]
        lanes = jnp.arange(NB, dtype=jnp.int32)
        row_live = lanes[None, :] < block_size[:, None]
        col_live = lanes[None, None, :] < block_size[nu_list][:, :, None]
        slot_live = jnp.arange(knu, dtype=jnp.int32)[None, :] < nu_count[:, None]
        mask = row_live[:, None, :, None] & col_live[:, :, None, :] & slot_live[:, :, None, None]
        blocks = three_center[0].reshape(aux_dev, n_mu, knu, NB, NB)
        masked = jnp.where(mask[None], blocks, jnp.zeros((), jnp.bfloat16))
        picked = occupied.reshape(n_mu, NB, n_occ)[nu_list]
        half = jnp.einsum(
            "qmkab,mkbi->qmai", masked, picked, preferred_element_type=jnp.float32
        ).astype(jnp.bfloat16)
        half = half.reshape(aux_dev, n_mu, NB * n_occ)
        regrouped = lax.all_to_all(half, "grp", split_axis=1, concat_axis=0, tiled=True)
        n_aux = regrouped.shape[0]
        mu_dev = regrouped.shape[1]
        regrouped = regrouped.reshape(n_aux, mu_dev, NB, n_occ)
        orbital = jnp.einsum(
            "pq,qmai->mapi", metric[0], regrouped, preferred_element_type=jnp.float32
        ).astype(jnp.bfloat16)
        rows = mu_dev * NB
        orbital = orbital.reshape(rows, n_aux * n_occ)
        hr = rows // 2
        me = lax.axis_index("grp")
        pos = jnp.asarray(pos_of)[me]
        ring_c = jnp.asarray(ring_arr)
        term = jnp.zeros((n * rows, rows), jnp.float32)

        def place(term, piece, src, off):
            part = jnp.dot(piece, orbital.T, preferred_element_type=jnp.float32)
            return lax.dynamic_update_slice_in_dim(term, part, src * rows + off, axis=0)

        term = place(term, orbital, me, 0)
        a = orbital[:hr]
        b = orbital[hr:]
        for k in range(1, n):
            a = lax.ppermute(a, "grp", fwd)
            term = place(term, a, ring_c[(pos - k) % n], 0)
            b = lax.ppermute(b, "grp", bwd)
            term = place(term, b, ring_c[(pos + k) % n], hr)
        return lax.psum_scatter(term, "rep", scatter_dimension=0, tiled=True)

    return body


def solution(mesh):
    return jax.shard_map(
        make_body(ring_order(mesh)),
        mesh=mesh,
        in_specs=(P("rep", "grp", None, None, None), P("rep", None, None), P(), P(), P(), P()),
        out_specs=P("rep", "grp"),
        check_vma=False,
    )
```

```python
import jax
import jax.numpy as jnp
import numpy as np
from jax import lax
from jax.sharding import PartitionSpec as P

NB = 64


def snake(a_size, b_size):
    if a_size % 2:
        return [(a, b) for b, a in snake(b_size, a_size)]
    if b_size == 1:
        return [(a, 0) for a in range(a_size)]
    path = []
    for a in range(a_size):
        cols = range(b_size) if a == 0 else (range(1, b_size) if a % 2 == 0 else range(b_size - 1, 0, -1))
        path += [(a, b) for b in cols]
    path += [(a, 0) for a in range(a_size - 1, 0, -1)]
    return path


def ring_order(mesh):
    n = mesh.shape["grp"]
    try:
        devs = np.asarray(mesh.devices).reshape(n, -1)[:, 0]
        coords = [tuple(d.coords) for d in devs]
    except (AttributeError, TypeError):
        return list(range(n))
    varying = [i for i in range(len(coords[0])) if len({c[i] for c in coords}) > 1]
    if len(varying) == 1:
        key = sorted(range(n), key=lambda g: coords[g][varying[0]])
        return key
    if len(varying) != 2:
        return list(range(n))
    i, j = varying
    avals = sorted({c[i] for c in coords})
    bvals = sorted({c[j] for c in coords})
    where = {(avals.index(c[i]), bvals.index(c[j])): g for g, c in enumerate(coords)}
    if len(where) != n:
        return list(range(n))
    return [where[p] for p in snake(len(avals), len(bvals))]


def make_body(ring):
    n = len(ring)
    pos_of = np.zeros(n, np.int32)
    for p, g in enumerate(ring):
        pos_of[g] = p
    ring_arr = np.asarray(ring, np.int32)

    def shifted(s):
        return [(ring[p], ring[(p + s) % n]) for p in range(n)]

    def body(three_center, metric, occupied, nu_list, nu_count, block_size):
        n_mu, knu = nu_list.shape
        n_occ = occupied.shape[1]
        aux_dev = three_center.shape[1]
        lanes = jnp.arange(NB, dtype=jnp.int32)
        row_live = lanes[None, :] < block_size[:, None]
        col_live = lanes[None, None, :] < block_size[nu_list][:, :, None]
        slot_live = jnp.arange(knu, dtype=jnp.int32)[None, :] < nu_count[:, None]
        mask = row_live[:, None, :, None] & col_live[:, :, None, :] & slot_live[:, :, None, None]
        blocks = three_center[0].reshape(aux_dev, n_mu, knu, NB, NB)
        masked = jnp.where(mask[None], blocks, jnp.zeros((), jnp.bfloat16))
        picked = occupied.reshape(n_mu, NB, n_occ)[nu_list]
        half = jnp.einsum(
            "qmkab,mkbi->qmai", masked, picked, preferred_element_type=jnp.float32
        ).astype(jnp.bfloat16)
        half = half.reshape(aux_dev, n_mu, NB * n_occ)
        regrouped = lax.all_to_all(half, "grp", split_axis=1, concat_axis=0, tiled=True)
        n_aux = regrouped.shape[0]
        mu_dev = regrouped.shape[1]
        regrouped = regrouped.reshape(n_aux, mu_dev, NB, n_occ)
        orbital = jnp.einsum(
            "pq,qmai->mapi", metric[0], regrouped, preferred_element_type=jnp.float32
        ).astype(jnp.bfloat16)
        rows = mu_dev * NB
        orbital = orbital.reshape(rows, n_aux * n_occ)
        me = lax.axis_index("grp")
        pos = jnp.asarray(pos_of)[me]
        ring_c = jnp.asarray(ring_arr)

        def start_of(off):
            return ring_c[(pos + off) % n] * rows

        radius = n // 4
        held = {0: orbital}
        fwd = orbital
        bwd = orbital
        for k in range(1, radius + 1):
            fwd = lax.ppermute(fwd, "grp", shifted(1))
            held[-k] = fwd
            bwd = lax.ppermute(bwd, "grp", shifted(-1))
            held[k] = bwd

        def prod(xo, yo):
            return jnp.dot(held[xo], held[yo].T, preferred_element_type=jnp.float32)

        local = []
        outgoing = {}
        for d in range(n // 2 + 1):
            xo = -((d + 1) // 2)
            yo = xo + d
            blk = prod(xo, yo)
            s = d // 2
            if s == 0:
                local.append((-d, blk))
            else:
                outgoing.setdefault(s, []).append((-d, blk))
            if 0 < d < n // 2:
                outgoing.setdefault(xo, []).append((d, blk.T))
        placed = list(local)
        for s, items in sorted(outgoing.items()):
            stack = jnp.stack([b for _, b in items])
            got = lax.ppermute(stack, "grp", shifted(s))
            placed += [(off, got[i]) for i, (off, _) in enumerate(items)]
        term = jnp.zeros((n * rows, rows), jnp.float32)
        for off, blk in placed:
            term = lax.dynamic_update_slice_in_dim(term, blk, start_of(off), axis=0)
        return lax.psum_scatter(term, "rep", scatter_dimension=0, tiled=True)

    return body


def solution(mesh):
    return jax.shard_map(
        make_body(ring_order(mesh)),
        mesh=mesh,
        in_specs=(P("rep", "grp", None, None, None), P("rep", None, None), P(), P(), P(), P()),
        out_specs=P("rep", "grp"),
        check_vma=False,
    )
```

```python
import jax
import jax.numpy as jnp
import numpy as np
from jax import lax
from jax.sharding import PartitionSpec as P

NB = 64


def snake(a_size, b_size):
    if a_size % 2:
        return [(a, b) for b, a in snake(b_size, a_size)]
    if b_size == 1:
        return [(a, 0) for a in range(a_size)]
    path = []
    for a in range(a_size):
        cols = range(b_size) if a == 0 else (range(1, b_size) if a % 2 == 0 else range(b_size - 1, 0, -1))
        path += [(a, b) for b in cols]
    path += [(a, 0) for a in range(a_size - 1, 0, -1)]
    return path


def ring_order(mesh):
    n = mesh.shape["grp"]
    try:
        devs = np.asarray(mesh.devices).reshape(n, -1)[:, 0]
        coords = [tuple(d.coords) for d in devs]
    except (AttributeError, TypeError):
        return list(range(n))
    varying = [i for i in range(len(coords[0])) if len({c[i] for c in coords}) > 1]
    if len(varying) == 1:
        key = sorted(range(n), key=lambda g: coords[g][varying[0]])
        return key
    if len(varying) != 2:
        return list(range(n))
    i, j = varying
    avals = sorted({c[i] for c in coords})
    bvals = sorted({c[j] for c in coords})
    where = {(avals.index(c[i]), bvals.index(c[j])): g for g, c in enumerate(coords)}
    if len(where) != n:
        return list(range(n))
    return [where[p] for p in snake(len(avals), len(bvals))]


def make_body(ring):
    n = len(ring)
    pos_of = np.zeros(n, np.int32)
    for p, g in enumerate(ring):
        pos_of[g] = p
    ring_arr = np.asarray(ring, np.int32)

    def shifted(s):
        return [(ring[p], ring[(p + s) % n]) for p in range(n)]

    def body(three_center, metric, occupied, nu_list, nu_count, block_size):
        n_mu, knu = nu_list.shape
        n_occ = occupied.shape[1]
        aux_dev = three_center.shape[1]
        lanes = jnp.arange(NB, dtype=jnp.int32)
        row_live = lanes[None, :] < block_size[:, None]
        col_live = lanes[None, None, :] < block_size[nu_list][:, :, None]
        slot_live = jnp.arange(knu, dtype=jnp.int32)[None, :] < nu_count[:, None]
        mask = row_live[:, None, :, None] & col_live[:, :, None, :] & slot_live[:, :, None, None]
        picked = occupied.reshape(n_mu, NB, n_occ)[nu_list]
        me = lax.axis_index("grp")
        pos = jnp.asarray(pos_of)[me]
        ring_c = jnp.asarray(ring_arr)
        mu_dev = n_mu // n
        tc = three_center[0]
        pieces = []
        for s in range(n):
            dest = ring_c[(pos + s) % n]
            m0 = dest * mu_dev
            chunk = lax.dynamic_slice_in_dim(tc, m0, mu_dev, axis=1)
            chunk = chunk.reshape(aux_dev, mu_dev, knu, NB, NB)
            live = lax.dynamic_slice_in_dim(mask, m0, mu_dev, axis=0)
            masked = jnp.where(live[None], chunk, jnp.zeros((), jnp.bfloat16))
            sel = lax.dynamic_slice_in_dim(picked, m0, mu_dev, axis=0)
            half = jnp.einsum(
                "qmkab,mkbi->qmai", masked, sel, preferred_element_type=jnp.float32
            ).astype(jnp.bfloat16)
            if s:
                half = lax.ppermute(half, "grp", shifted(s))
            pieces.append(half)
        regrouped = jnp.zeros((n * aux_dev, mu_dev, NB, n_occ), jnp.bfloat16)
        for s, half in enumerate(pieces):
            src_g = ring_c[(pos - s) % n]
            regrouped = lax.dynamic_update_slice_in_dim(regrouped, half, src_g * aux_dev, axis=0)
        n_aux = regrouped.shape[0]
        mu_dev = regrouped.shape[1]
        regrouped = regrouped.reshape(n_aux, mu_dev, NB, n_occ)
        orbital = jnp.einsum(
            "pq,qmai->mapi", metric[0], regrouped, preferred_element_type=jnp.float32
        ).astype(jnp.bfloat16)
        rows = mu_dev * NB
        orbital = orbital.reshape(rows, n_aux * n_occ)

        def start_of(off):
            return ring_c[(pos + off) % n] * rows

        radius = n // 4
        held = {0: orbital}
        fwd = orbital
        bwd = orbital
        for k in range(1, radius + 1):
            fwd = lax.ppermute(fwd, "grp", shifted(1))
            held[-k] = fwd
            bwd = lax.ppermute(bwd, "grp", shifted(-1))
            held[k] = bwd

        def prod(xo, yo):
            return jnp.dot(held[xo], held[yo].T, preferred_element_type=jnp.float32)

        local = []
        outgoing = {}
        for d in range(n // 2 + 1):
            xo = -((d + 1) // 2)
            yo = xo + d
            blk = prod(xo, yo)
            s = d // 2
            if s == 0:
                local.append((-d, blk))
            else:
                outgoing.setdefault(s, []).append((-d, blk))
            if 0 < d < n // 2:
                outgoing.setdefault(xo, []).append((d, blk.T))
        placed = list(local)
        for s, items in sorted(outgoing.items()):
            stack = jnp.stack([b for _, b in items])
            got = lax.ppermute(stack, "grp", shifted(s))
            placed += [(off, got[i]) for i, (off, _) in enumerate(items)]
        term = jnp.zeros((n * rows, rows), jnp.float32)
        for off, blk in placed:
            term = lax.dynamic_update_slice_in_dim(term, blk, start_of(off), axis=0)
        return lax.psum_scatter(term, "rep", scatter_dimension=0, tiled=True)

    return body


def solution(mesh):
    return jax.shard_map(
        make_body(ring_order(mesh)),
        mesh=mesh,
        in_specs=(P("rep", "grp", None, None, None), P("rep", None, None), P(), P(), P(), P()),
        out_specs=P("rep", "grp"),
        check_vma=False,
    )
```

```python
import jax
import jax.numpy as jnp
import numpy as np
from jax import lax
from jax.sharding import PartitionSpec as P

NB = 64


def snake(a_size, b_size):
    if a_size % 2:
        return [(a, b) for b, a in snake(b_size, a_size)]
    if b_size == 1:
        return [(a, 0) for a in range(a_size)]
    path = []
    for a in range(a_size):
        cols = range(b_size) if a == 0 else (range(1, b_size) if a % 2 == 0 else range(b_size - 1, 0, -1))
        path += [(a, b) for b in cols]
    path += [(a, 0) for a in range(a_size - 1, 0, -1)]
    return path


def ring_order(mesh):
    n = mesh.shape["grp"]
    try:
        devs = np.asarray(mesh.devices).reshape(n, -1)[:, 0]
        coords = [tuple(d.coords) for d in devs]
    except (AttributeError, TypeError):
        return list(range(n))
    varying = [i for i in range(len(coords[0])) if len({c[i] for c in coords}) > 1]
    if len(varying) == 1:
        key = sorted(range(n), key=lambda g: coords[g][varying[0]])
        return key
    if len(varying) != 2:
        return list(range(n))
    i, j = varying
    avals = sorted({c[i] for c in coords})
    bvals = sorted({c[j] for c in coords})
    where = {(avals.index(c[i]), bvals.index(c[j])): g for g, c in enumerate(coords)}
    if len(where) != n:
        return list(range(n))
    return [where[p] for p in snake(len(avals), len(bvals))]


def make_body(ring):
    n = len(ring)
    pos_of = np.zeros(n, np.int32)
    for p, g in enumerate(ring):
        pos_of[g] = p
    ring_arr = np.asarray(ring, np.int32)

    def shifted(s):
        return [(ring[p], ring[(p + s) % n]) for p in range(n)]

    def body(three_center, metric, occupied, nu_list, nu_count, block_size):
        n_mu, knu = nu_list.shape
        n_occ = occupied.shape[1]
        aux_dev = three_center.shape[1]
        lanes = jnp.arange(NB, dtype=jnp.int32)
        row_live = lanes[None, :] < block_size[:, None]
        col_live = lanes[None, None, :] < block_size[nu_list][:, :, None]
        slot_live = jnp.arange(knu, dtype=jnp.int32)[None, :] < nu_count[:, None]
        mask = row_live[:, None, :, None] & col_live[:, :, None, :] & slot_live[:, :, None, None]
        picked = occupied.reshape(n_mu, NB, n_occ)[nu_list]
        me = lax.axis_index("grp")
        pos = jnp.asarray(pos_of)[me]
        ring_c = jnp.asarray(ring_arr)
        mu_dev = n_mu // n
        tc = three_center[0]
        pieces = []
        for s in range(n):
            dest = ring_c[(pos + s) % n]
            m0 = dest * mu_dev
            chunk = lax.dynamic_slice_in_dim(tc, m0, mu_dev, axis=1)
            chunk = chunk.reshape(aux_dev, mu_dev, knu, NB, NB)
            live = lax.dynamic_slice_in_dim(mask, m0, mu_dev, axis=0)
            masked = jnp.where(live[None], chunk, jnp.zeros((), jnp.bfloat16))
            sel = lax.dynamic_slice_in_dim(picked, m0, mu_dev, axis=0)
            half = jnp.einsum(
                "qmkab,mkbi->qmai", masked, sel, preferred_element_type=jnp.float32
            ).astype(jnp.bfloat16)
            if s:
                half = lax.ppermute(half, "grp", shifted(s))
            pieces.append(half)
        stacked = jnp.stack(pieces)
        srcs = ring_c[(pos - jnp.arange(n, dtype=jnp.int32)) % n]
        cols = (srcs[:, None] * aux_dev + jnp.arange(aux_dev, dtype=jnp.int32)[None, :]).reshape(-1)
        factor = jnp.take(metric[0], cols, axis=1).reshape(-1, n, aux_dev)
        orbital = jnp.einsum(
            "psq,sqmai->mapi", factor, stacked, preferred_element_type=jnp.float32
        ).astype(jnp.bfloat16)
        n_aux = n * aux_dev
        rows = mu_dev * NB
        orbital = orbital.reshape(rows, n_aux * n_occ)

        def start_of(off):
            return ring_c[(pos + off) % n] * rows

        radius = n // 4
        held = {0: orbital}
        fwd = orbital
        bwd = orbital
        for k in range(1, radius + 1):
            fwd = lax.ppermute(fwd, "grp", shifted(1))
            held[-k] = fwd
            bwd = lax.ppermute(bwd, "grp", shifted(-1))
            held[k] = bwd

        def prod(xo, yo):
            return jnp.dot(held[xo], held[yo].T, preferred_element_type=jnp.float32)

        local = []
        outgoing = {}
        for d in range(n // 2 + 1):
            xo = -((d + 1) // 2)
            yo = xo + d
            blk = prod(xo, yo)
            s = d // 2
            if s == 0:
                local.append((-d, blk))
            else:
                outgoing.setdefault(s, []).append((-d, blk))
            if 0 < d < n // 2:
                outgoing.setdefault(xo, []).append((d, blk.T))
        placed = list(local)
        for s, items in sorted(outgoing.items()):
            stack = jnp.stack([b for _, b in items])
            got = lax.ppermute(stack, "grp", shifted(s))
            placed += [(off, got[i]) for i, (off, _) in enumerate(items)]
        term = jnp.zeros((n * rows, rows), jnp.float32)
        for off, blk in placed:
            term = lax.dynamic_update_slice_in_dim(term, blk, start_of(off), axis=0)
        return lax.psum_scatter(term, "rep", scatter_dimension=0, tiled=True)

    return body


def solution(mesh):
    return jax.shard_map(
        make_body(ring_order(mesh)),
        mesh=mesh,
        in_specs=(P("rep", "grp", None, None, None), P("rep", None, None), P(), P(), P(), P()),
        out_specs=P("rep", "grp"),
        check_vma=False,
    )
```

```python
import jax
import jax.numpy as jnp
import numpy as np
from jax import lax
from jax.sharding import PartitionSpec as P

NB = 64


def snake(a_size, b_size):
    if a_size % 2:
        return [(a, b) for b, a in snake(b_size, a_size)]
    if b_size == 1:
        return [(a, 0) for a in range(a_size)]
    path = []
    for a in range(a_size):
        cols = range(b_size) if a == 0 else (range(1, b_size) if a % 2 == 0 else range(b_size - 1, 0, -1))
        path += [(a, b) for b in cols]
    path += [(a, 0) for a in range(a_size - 1, 0, -1)]
    return path


def ring_order(mesh):
    n = mesh.shape["grp"]
    try:
        devs = np.asarray(mesh.devices).reshape(n, -1)[:, 0]
        coords = [tuple(d.coords) for d in devs]
    except (AttributeError, TypeError):
        return list(range(n))
    varying = [i for i in range(len(coords[0])) if len({c[i] for c in coords}) > 1]
    if len(varying) == 1:
        key = sorted(range(n), key=lambda g: coords[g][varying[0]])
        return key
    if len(varying) != 2:
        return list(range(n))
    i, j = varying
    avals = sorted({c[i] for c in coords})
    bvals = sorted({c[j] for c in coords})
    where = {(avals.index(c[i]), bvals.index(c[j])): g for g, c in enumerate(coords)}
    if len(where) != n:
        return list(range(n))
    return [where[p] for p in snake(len(avals), len(bvals))]


def make_body(ring):
    n = len(ring)
    pos_of = np.zeros(n, np.int32)
    for p, g in enumerate(ring):
        pos_of[g] = p
    ring_arr = np.asarray(ring, np.int32)

    def shifted(s):
        return [(ring[p], ring[(p + s) % n]) for p in range(n)]

    def body(three_center, metric, occupied, nu_list, nu_count, block_size):
        n_mu, knu = nu_list.shape
        n_occ = occupied.shape[1]
        aux_dev = three_center.shape[1]
        lanes = jnp.arange(NB, dtype=jnp.int32)
        row_live = lanes[None, :] < block_size[:, None]
        col_live = lanes[None, None, :] < block_size[nu_list][:, :, None]
        slot_live = jnp.arange(knu, dtype=jnp.int32)[None, :] < nu_count[:, None]
        keep = col_live & slot_live[:, :, None]
        picked = occupied.reshape(n_mu, NB, n_occ)[nu_list]
        picked = jnp.where(keep[..., None], picked, jnp.zeros((), jnp.bfloat16))
        pair = 2
        eye = jnp.eye(pair, dtype=jnp.bfloat16)
        weight = jnp.einsum("xy,mkbi->mkxbyi", eye, picked).reshape(n_mu, knu, pair * NB, pair * n_occ)
        tiles = NB // pair
        tc = jnp.swapaxes(three_center[0], 1, 2).reshape(aux_dev, knu, n_mu, tiles, pair * NB)
        half = jnp.einsum("qkmtl,mklc->qmtc", tc, weight, preferred_element_type=jnp.float32)
        half = half.reshape(aux_dev, n_mu, NB, n_occ)
        half = jnp.where(row_live[None, :, :, None], half, 0.0).astype(jnp.bfloat16)
        half = half.reshape(aux_dev, n_mu, NB * n_occ)
        regrouped = lax.all_to_all(half, "grp", split_axis=1, concat_axis=0, tiled=True)
        n_aux = regrouped.shape[0]
        mu_dev = regrouped.shape[1]
        regrouped = regrouped.reshape(n_aux, mu_dev, NB, n_occ)
        orbital = jnp.einsum(
            "pq,qmai->mapi", metric[0], regrouped, preferred_element_type=jnp.float32
        ).astype(jnp.bfloat16)
        rows = mu_dev * NB
        orbital = orbital.reshape(rows, n_aux * n_occ)
        me = lax.axis_index("grp")
        pos = jnp.asarray(pos_of)[me]
        ring_c = jnp.asarray(ring_arr)

        def start_of(off):
            return ring_c[(pos + off) % n] * rows

        radius = n // 4
        held = {0: orbital}
        fwd = orbital
        bwd = orbital
        for k in range(1, radius + 1):
            fwd = lax.ppermute(fwd, "grp", shifted(1))
            held[-k] = fwd
            bwd = lax.ppermute(bwd, "grp", shifted(-1))
            held[k] = bwd

        def prod(xo, yo):
            return jnp.dot(held[xo], held[yo].T, preferred_element_type=jnp.float32)

        local = []
        outgoing = {}
        for d in range(n // 2 + 1):
            xo = -((d + 1) // 2)
            yo = xo + d
            blk = prod(xo, yo)
            s = d // 2
            if s == 0:
                local.append((-d, blk))
            else:
                outgoing.setdefault(s, []).append((-d, blk))
            if 0 < d < n // 2:
                outgoing.setdefault(xo, []).append((d, blk.T))
        placed = list(local)
        for s, items in sorted(outgoing.items()):
            stack = jnp.stack([b for _, b in items])
            got = lax.ppermute(stack, "grp", shifted(s))
            placed += [(off, got[i]) for i, (off, _) in enumerate(items)]
        term = jnp.zeros((n * rows, rows), jnp.float32)
        for off, blk in placed:
            term = lax.dynamic_update_slice_in_dim(term, blk, start_of(off), axis=0)
        return lax.psum_scatter(term, "rep", scatter_dimension=0, tiled=True)

    return body


def solution(mesh):
    return jax.shard_map(
        make_body(ring_order(mesh)),
        mesh=mesh,
        in_specs=(P("rep", "grp", None, None, None), P("rep", None, None), P(), P(), P(), P()),
        out_specs=P("rep", "grp"),
        check_vma=False,
    )
```

```python
import jax
import jax.numpy as jnp
import numpy as np
from jax import lax
from jax.sharding import PartitionSpec as P

NB = 64


def snake(a_size, b_size):
    if a_size % 2:
        return [(a, b) for b, a in snake(b_size, a_size)]
    if b_size == 1:
        return [(a, 0) for a in range(a_size)]
    path = []
    for a in range(a_size):
        cols = range(b_size) if a == 0 else (range(1, b_size) if a % 2 == 0 else range(b_size - 1, 0, -1))
        path += [(a, b) for b in cols]
    path += [(a, 0) for a in range(a_size - 1, 0, -1)]
    return path


def ring_order(mesh):
    n = mesh.shape["grp"]
    try:
        devs = np.asarray(mesh.devices).reshape(n, -1)[:, 0]
        coords = [tuple(d.coords) for d in devs]
    except (AttributeError, TypeError):
        return list(range(n))
    varying = [i for i in range(len(coords[0])) if len({c[i] for c in coords}) > 1]
    if len(varying) == 1:
        key = sorted(range(n), key=lambda g: coords[g][varying[0]])
        return key
    if len(varying) != 2:
        return list(range(n))
    i, j = varying
    avals = sorted({c[i] for c in coords})
    bvals = sorted({c[j] for c in coords})
    where = {(avals.index(c[i]), bvals.index(c[j])): g for g, c in enumerate(coords)}
    if len(where) != n:
        return list(range(n))
    return [where[p] for p in snake(len(avals), len(bvals))]


def make_body(ring):
    n = len(ring)
    pos_of = np.zeros(n, np.int32)
    for p, g in enumerate(ring):
        pos_of[g] = p
    ring_arr = np.asarray(ring, np.int32)

    def shifted(s):
        return [(ring[p], ring[(p + s) % n]) for p in range(n)]

    def body(three_center, metric, occupied, nu_list, nu_count, block_size):
        n_mu, knu = nu_list.shape
        n_occ = occupied.shape[1]
        aux_dev = three_center.shape[1]
        lanes = jnp.arange(NB, dtype=jnp.int32)
        row_live = lanes[None, :] < block_size[:, None]
        col_live = lanes[None, None, :] < block_size[nu_list][:, :, None]
        slot_live = jnp.arange(knu, dtype=jnp.int32)[None, :] < nu_count[:, None]
        keep = col_live & slot_live[:, :, None]
        picked = occupied.reshape(n_mu, NB, n_occ)[nu_list]
        picked = jnp.where(keep[..., None], picked, jnp.zeros((), jnp.bfloat16))
        pair = 2
        blank = jnp.zeros_like(picked)
        weight = jnp.concatenate(
            [jnp.concatenate([picked, blank], axis=-1), jnp.concatenate([blank, picked], axis=-1)], axis=-2
        )
        tiles = NB // pair
        tc = jnp.swapaxes(three_center[0], 1, 2).reshape(aux_dev, knu, n_mu, tiles, pair * NB)
        half = jnp.einsum("qkmtl,mklc->qmtc", tc, weight, preferred_element_type=jnp.float32)
        half = half.reshape(aux_dev, n_mu, NB, n_occ)
        half = jnp.where(row_live[None, :, :, None], half, 0.0).astype(jnp.bfloat16)
        half = half.reshape(aux_dev, n_mu, NB * n_occ)
        regrouped = lax.all_to_all(half, "grp", split_axis=1, concat_axis=0, tiled=True)
        n_aux = regrouped.shape[0]
        mu_dev = regrouped.shape[1]
        regrouped = regrouped.reshape(n_aux, mu_dev, NB, n_occ)
        orbital = jnp.einsum(
            "pq,qmai->mapi", metric[0], regrouped, preferred_element_type=jnp.float32
        ).astype(jnp.bfloat16)
        rows = mu_dev * NB
        orbital = orbital.reshape(rows, n_aux * n_occ)
        me = lax.axis_index("grp")
        pos = jnp.asarray(pos_of)[me]
        ring_c = jnp.asarray(ring_arr)

        def start_of(off):
            return ring_c[(pos + off) % n] * rows

        radius = n // 4
        held = {0: orbital}
        fwd = orbital
        bwd = orbital
        for k in range(1, radius + 1):
            fwd = lax.ppermute(fwd, "grp", shifted(1))
            held[-k] = fwd
            bwd = lax.ppermute(bwd, "grp", shifted(-1))
            held[k] = bwd

        def prod(xo, yo):
            return jnp.dot(held[xo], held[yo].T, preferred_element_type=jnp.float32)

        local = []
        outgoing = {}
        for d in range(n // 2 + 1):
            xo = -((d + 1) // 2)
            yo = xo + d
            blk = prod(xo, yo)
            s = d // 2
            if s == 0:
                local.append((-d, blk))
            else:
                outgoing.setdefault(s, []).append((-d, blk))
            if 0 < d < n // 2:
                outgoing.setdefault(xo, []).append((d, blk.T))
        placed = list(local)
        for s, items in sorted(outgoing.items()):
            stack = jnp.stack([b for _, b in items])
            got = lax.ppermute(stack, "grp", shifted(s))
            placed += [(off, got[i]) for i, (off, _) in enumerate(items)]
        term = jnp.zeros((n * rows, rows), jnp.float32)
        for off, blk in placed:
            term = lax.dynamic_update_slice_in_dim(term, blk, start_of(off), axis=0)
        return lax.psum_scatter(term, "rep", scatter_dimension=0, tiled=True)

    return body


def solution(mesh):
    return jax.shard_map(
        make_body(ring_order(mesh)),
        mesh=mesh,
        in_specs=(P("rep", "grp", None, None, None), P("rep", None, None), P(), P(), P(), P()),
        out_specs=P("rep", "grp"),
        check_vma=False,
    )
```

```python
import jax
import jax.numpy as jnp
import numpy as np
from jax import lax
from jax.sharding import PartitionSpec as P

NB = 64


def snake(a_size, b_size):
    if a_size % 2:
        return [(a, b) for b, a in snake(b_size, a_size)]
    if b_size == 1:
        return [(a, 0) for a in range(a_size)]
    path = []
    for a in range(a_size):
        cols = range(b_size) if a == 0 else (range(1, b_size) if a % 2 == 0 else range(b_size - 1, 0, -1))
        path += [(a, b) for b in cols]
    path += [(a, 0) for a in range(a_size - 1, 0, -1)]
    return path


def ring_order(mesh):
    n = mesh.shape["grp"]
    try:
        devs = np.asarray(mesh.devices).reshape(n, -1)[:, 0]
        coords = [tuple(d.coords) for d in devs]
    except (AttributeError, TypeError):
        return list(range(n))
    varying = [i for i in range(len(coords[0])) if len({c[i] for c in coords}) > 1]
    if len(varying) == 1:
        key = sorted(range(n), key=lambda g: coords[g][varying[0]])
        return key
    if len(varying) != 2:
        return list(range(n))
    i, j = varying
    avals = sorted({c[i] for c in coords})
    bvals = sorted({c[j] for c in coords})
    where = {(avals.index(c[i]), bvals.index(c[j])): g for g, c in enumerate(coords)}
    if len(where) != n:
        return list(range(n))
    return [where[p] for p in snake(len(avals), len(bvals))]


def scatter_sum(term):
    n_rep = lax.axis_size("rep")
    if n_rep & (n_rep - 1):
        return lax.psum_scatter(term, "rep", scatter_dimension=0, tiled=True)
    me = lax.axis_index("rep")
    per = term.shape[0] // n_rep
    buf = term
    d = n_rep // 2
    while d >= 1:
        upper = (me // d) % 2
        keep = lax.dynamic_slice_in_dim(buf, upper * d * per, d * per, axis=0)
        send = lax.dynamic_slice_in_dim(buf, (1 - upper) * d * per, d * per, axis=0)
        got = lax.ppermute(send, "rep", [(i, i ^ d) for i in range(n_rep)])
        buf = keep + got
        d //= 2
    return buf


def make_body(ring):
    n = len(ring)
    pos_of = np.zeros(n, np.int32)
    for p, g in enumerate(ring):
        pos_of[g] = p
    ring_arr = np.asarray(ring, np.int32)

    def shifted(s):
        return [(ring[p], ring[(p + s) % n]) for p in range(n)]

    def body(three_center, metric, occupied, nu_list, nu_count, block_size):
        n_mu, knu = nu_list.shape
        n_occ = occupied.shape[1]
        aux_dev = three_center.shape[1]
        lanes = jnp.arange(NB, dtype=jnp.int32)
        row_live = lanes[None, :] < block_size[:, None]
        col_live = lanes[None, None, :] < block_size[nu_list][:, :, None]
        slot_live = jnp.arange(knu, dtype=jnp.int32)[None, :] < nu_count[:, None]
        keep = col_live & slot_live[:, :, None]
        picked = occupied.reshape(n_mu, NB, n_occ)[nu_list]
        picked = jnp.where(keep[..., None], picked, jnp.zeros((), jnp.bfloat16))
        pair = 2
        blank = jnp.zeros_like(picked)
        weight = jnp.concatenate(
            [jnp.concatenate([picked, blank], axis=-1), jnp.concatenate([blank, picked], axis=-1)], axis=-2
        )
        tiles = NB // pair
        tc = jnp.swapaxes(three_center[0], 1, 2).reshape(aux_dev, knu, n_mu, tiles, pair * NB)
        half = jnp.einsum("qkmtl,mklc->qmtc", tc, weight, preferred_element_type=jnp.float32)
        half = half.reshape(aux_dev, n_mu, NB, n_occ)
        half = jnp.where(row_live[None, :, :, None], half, 0.0).astype(jnp.bfloat16)
        half = half.reshape(aux_dev, n_mu, NB * n_occ)
        regrouped = lax.all_to_all(half, "grp", split_axis=1, concat_axis=0, tiled=True)
        n_aux = regrouped.shape[0]
        mu_dev = regrouped.shape[1]
        regrouped = regrouped.reshape(n_aux, mu_dev, NB, n_occ)
        orbital = jnp.einsum(
            "pq,qmai->mapi", metric[0], regrouped, preferred_element_type=jnp.float32
        ).astype(jnp.bfloat16)
        rows = mu_dev * NB
        orbital = orbital.reshape(rows, n_aux * n_occ)
        me = lax.axis_index("grp")
        pos = jnp.asarray(pos_of)[me]
        ring_c = jnp.asarray(ring_arr)

        def start_of(off):
            return ring_c[(pos + off) % n] * rows

        radius = n // 4
        held = {0: orbital}
        fwd = orbital
        bwd = orbital
        for k in range(1, radius + 1):
            fwd = lax.ppermute(fwd, "grp", shifted(1))
            held[-k] = fwd
            bwd = lax.ppermute(bwd, "grp", shifted(-1))
            held[k] = bwd

        def prod(xo, yo):
            return jnp.dot(held[xo], held[yo].T, preferred_element_type=jnp.float32)

        local = []
        outgoing = {}
        for d in range(n // 2 + 1):
            xo = -((d + 1) // 2)
            yo = xo + d
            blk = prod(xo, yo)
            s = d // 2
            if s == 0:
                local.append((-d, blk))
            else:
                outgoing.setdefault(s, []).append((-d, blk))
            if 0 < d < n // 2:
                outgoing.setdefault(xo, []).append((d, blk.T))
        placed = list(local)
        for s, items in sorted(outgoing.items()):
            stack = jnp.stack([b for _, b in items])
            got = lax.ppermute(stack, "grp", shifted(s))
            placed += [(off, got[i]) for i, (off, _) in enumerate(items)]
        term = jnp.zeros((n * rows, rows), jnp.float32)
        for off, blk in placed:
            term = lax.dynamic_update_slice_in_dim(term, blk, start_of(off), axis=0)
        return scatter_sum(term)

    return body


def solution(mesh):
    return jax.shard_map(
        make_body(ring_order(mesh)),
        mesh=mesh,
        in_specs=(P("rep", "grp", None, None, None), P("rep", None, None), P(), P(), P(), P()),
        out_specs=P("rep", "grp"),
        check_vma=False,
    )
```

```python
import jax
import jax.numpy as jnp
import numpy as np
from jax import lax
from jax.sharding import PartitionSpec as P

NB = 64


def snake(a_size, b_size):
    if a_size % 2:
        return [(a, b) for b, a in snake(b_size, a_size)]
    if b_size == 1:
        return [(a, 0) for a in range(a_size)]
    path = []
    for a in range(a_size):
        cols = range(b_size) if a == 0 else (range(1, b_size) if a % 2 == 0 else range(b_size - 1, 0, -1))
        path += [(a, b) for b in cols]
    path += [(a, 0) for a in range(a_size - 1, 0, -1)]
    return path


def ring_order(mesh):
    n = mesh.shape["grp"]
    try:
        devs = np.asarray(mesh.devices).reshape(n, -1)[:, 0]
        coords = [tuple(d.coords) for d in devs]
    except (AttributeError, TypeError):
        return list(range(n))
    varying = [i for i in range(len(coords[0])) if len({c[i] for c in coords}) > 1]
    if len(varying) == 1:
        key = sorted(range(n), key=lambda g: coords[g][varying[0]])
        return key
    if len(varying) != 2:
        return list(range(n))
    i, j = varying
    avals = sorted({c[i] for c in coords})
    bvals = sorted({c[j] for c in coords})
    where = {(avals.index(c[i]), bvals.index(c[j])): g for g, c in enumerate(coords)}
    if len(where) != n:
        return list(range(n))
    return [where[p] for p in snake(len(avals), len(bvals))]


def scatter_sum(term):
    n_rep = lax.axis_size("rep")
    if n_rep & (n_rep - 1):
        return lax.psum_scatter(term, "rep", scatter_dimension=0, tiled=True)
    me = lax.axis_index("rep")
    per = term.shape[0] // n_rep
    buf = term
    d = n_rep // 2
    while d >= 1:
        upper = (me // d) % 2
        keep = lax.dynamic_slice_in_dim(buf, upper * d * per, d * per, axis=0)
        send = lax.dynamic_slice_in_dim(buf, (1 - upper) * d * per, d * per, axis=0)
        got = lax.ppermute(send, "rep", [(i, i ^ d) for i in range(n_rep)])
        buf = keep + got
        d //= 2
    return buf


def make_body(ring):
    n = len(ring)
    pos_of = np.zeros(n, np.int32)
    for p, g in enumerate(ring):
        pos_of[g] = p
    ring_arr = np.asarray(ring, np.int32)

    def shifted(s):
        return [(ring[p], ring[(p + s) % n]) for p in range(n)]

    def body(three_center, metric, occupied, nu_list, nu_count, block_size):
        n_mu, knu = nu_list.shape
        n_occ = occupied.shape[1]
        aux_dev = three_center.shape[1]
        lanes = jnp.arange(NB, dtype=jnp.int32)
        row_live = lanes[None, :] < block_size[:, None]
        col_live = lanes[None, None, :] < block_size[nu_list][:, :, None]
        slot_live = jnp.arange(knu, dtype=jnp.int32)[None, :] < nu_count[:, None]
        keep = col_live & slot_live[:, :, None]
        picked = occupied.reshape(n_mu, NB, n_occ)[nu_list]
        picked = jnp.where(keep[..., None], picked, jnp.zeros((), jnp.bfloat16))
        pair = 2
        blank = jnp.zeros_like(picked)
        weight = jnp.concatenate(
            [jnp.concatenate([picked, blank], axis=-1), jnp.concatenate([blank, picked], axis=-1)], axis=-2
        )
        tiles = NB // pair
        tc = jnp.swapaxes(three_center[0], 1, 2).reshape(aux_dev, knu, n_mu, tiles, pair * NB)
        weight = weight.reshape(n_mu, knu, pair * NB, pair, n_occ)
        half = jnp.einsum("qkmtl,mklai->qimta", tc, weight, preferred_element_type=jnp.float32)
        half = half.reshape(aux_dev, n_occ, n_mu, NB)
        half = jnp.where(row_live[None, None], half, 0.0).astype(jnp.bfloat16)
        mu_dev = n_mu // n
        rows = mu_dev * NB
        half = half.reshape(aux_dev, n_occ, n, rows).transpose(2, 0, 1, 3)
        regrouped = lax.all_to_all(half, "grp", split_axis=0, concat_axis=0, tiled=True)
        n_aux = n * aux_dev
        regrouped = regrouped.reshape(n_aux, n_occ * rows)
        orbital = jnp.dot(metric[0], regrouped, preferred_element_type=jnp.float32).astype(jnp.bfloat16)
        orbital = orbital.reshape(n_aux * n_occ, rows)
        me = lax.axis_index("grp")
        pos = jnp.asarray(pos_of)[me]
        ring_c = jnp.asarray(ring_arr)

        def start_of(off):
            return ring_c[(pos + off) % n] * rows

        radius = n // 4
        held = {0: orbital}
        fwd = orbital
        bwd = orbital
        for k in range(1, radius + 1):
            fwd = lax.ppermute(fwd, "grp", shifted(1))
            held[-k] = fwd
            bwd = lax.ppermute(bwd, "grp", shifted(-1))
            held[k] = bwd

        def prod(xo, yo):
            return lax.dot_general(
                held[xo], held[yo], (((0,), (0,)), ((), ())), preferred_element_type=jnp.float32
            )

        local = []
        outgoing = {}
        for d in range(n // 2 + 1):
            xo = -((d + 1) // 2)
            yo = xo + d
            blk = prod(xo, yo)
            s = d // 2
            if s == 0:
                local.append((-d, blk))
            else:
                outgoing.setdefault(s, []).append((-d, blk))
            if 0 < d < n // 2:
                outgoing.setdefault(xo, []).append((d, blk.T))
        placed = list(local)
        for s, items in sorted(outgoing.items()):
            stack = jnp.stack([b for _, b in items])
            got = lax.ppermute(stack, "grp", shifted(s))
            placed += [(off, got[i]) for i, (off, _) in enumerate(items)]
        term = jnp.zeros((n * rows, rows), jnp.float32)
        for off, blk in placed:
            term = lax.dynamic_update_slice_in_dim(term, blk, start_of(off), axis=0)
        return scatter_sum(term)

    return body


def solution(mesh):
    return jax.shard_map(
        make_body(ring_order(mesh)),
        mesh=mesh,
        in_specs=(P("rep", "grp", None, None, None), P("rep", None, None), P(), P(), P(), P()),
        out_specs=P("rep", "grp"),
        check_vma=False,
    )
```

```python
import jax
import jax.numpy as jnp
import numpy as np
from jax import lax
from jax.sharding import PartitionSpec as P

NB = 64


def snake(a_size, b_size):
    if a_size % 2:
        return [(a, b) for b, a in snake(b_size, a_size)]
    if b_size == 1:
        return [(a, 0) for a in range(a_size)]
    path = []
    for a in range(a_size):
        cols = range(b_size) if a == 0 else (range(1, b_size) if a % 2 == 0 else range(b_size - 1, 0, -1))
        path += [(a, b) for b in cols]
    path += [(a, 0) for a in range(a_size - 1, 0, -1)]
    return path


def ring_order(mesh):
    n = mesh.shape["grp"]
    try:
        devs = np.asarray(mesh.devices).reshape(n, -1)[:, 0]
        coords = [tuple(d.coords) for d in devs]
    except (AttributeError, TypeError):
        return list(range(n))
    varying = [i for i in range(len(coords[0])) if len({c[i] for c in coords}) > 1]
    if len(varying) == 1:
        key = sorted(range(n), key=lambda g: coords[g][varying[0]])
        return key
    if len(varying) != 2:
        return list(range(n))
    i, j = varying
    avals = sorted({c[i] for c in coords})
    bvals = sorted({c[j] for c in coords})
    where = {(avals.index(c[i]), bvals.index(c[j])): g for g, c in enumerate(coords)}
    if len(where) != n:
        return list(range(n))
    return [where[p] for p in snake(len(avals), len(bvals))]


def scatter_sum(term):
    n_rep = lax.axis_size("rep")
    if n_rep & (n_rep - 1):
        return lax.psum_scatter(term, "rep", scatter_dimension=0, tiled=True)
    me = lax.axis_index("rep")
    bits = n_rep.bit_length() - 1
    per = term.shape[0] // n_rep
    buf = term.reshape((2,) * bits + (per,) + term.shape[1:])
    for b in range(bits):
        d = 1 << b
        axis = buf.ndim - 3
        mine = (me // d) % 2
        keep = lax.dynamic_index_in_dim(buf, mine, axis=axis, keepdims=False)
        send = lax.dynamic_index_in_dim(buf, 1 - mine, axis=axis, keepdims=False)
        got = lax.ppermute(send, "rep", [(i, i ^ d) for i in range(n_rep)])
        buf = keep + got
    return buf.reshape(per, term.shape[1])


def make_body(ring):
    n = len(ring)
    pos_of = np.zeros(n, np.int32)
    for p, g in enumerate(ring):
        pos_of[g] = p
    ring_arr = np.asarray(ring, np.int32)

    def shifted(s):
        return [(ring[p], ring[(p + s) % n]) for p in range(n)]

    def body(three_center, metric, occupied, nu_list, nu_count, block_size):
        n_mu, knu = nu_list.shape
        n_occ = occupied.shape[1]
        aux_dev = three_center.shape[1]
        lanes = jnp.arange(NB, dtype=jnp.int32)
        row_live = lanes[None, :] < block_size[:, None]
        col_live = lanes[None, None, :] < block_size[nu_list][:, :, None]
        slot_live = jnp.arange(knu, dtype=jnp.int32)[None, :] < nu_count[:, None]
        keep = col_live & slot_live[:, :, None]
        picked = occupied.reshape(n_mu, NB, n_occ)[nu_list]
        picked = jnp.where(keep[..., None], picked, jnp.zeros((), jnp.bfloat16))
        pair = 2
        blank = jnp.zeros_like(picked)
        weight = jnp.concatenate(
            [jnp.concatenate([picked, blank], axis=-1), jnp.concatenate([blank, picked], axis=-1)], axis=-2
        )
        tiles = NB // pair
        tc = jnp.swapaxes(three_center[0], 1, 2).reshape(aux_dev, knu, n_mu, tiles, pair * NB)
        half = jnp.einsum("qkmtl,mklc->qmtc", tc, weight, preferred_element_type=jnp.float32)
        half = half.reshape(aux_dev, n_mu, NB, n_occ)
        half = jnp.where(row_live[None, :, :, None], half, 0.0).astype(jnp.bfloat16)
        half = half.reshape(aux_dev, n_mu, NB * n_occ)
        regrouped = lax.all_to_all(half, "grp", split_axis=1, concat_axis=0, tiled=True)
        n_aux = regrouped.shape[0]
        mu_dev = regrouped.shape[1]
        regrouped = regrouped.reshape(n_aux, mu_dev, NB, n_occ)
        orbital = jnp.einsum(
            "pq,qmai->mapi", metric[0], regrouped, preferred_element_type=jnp.float32
        ).astype(jnp.bfloat16)
        rows = mu_dev * NB
        orbital = orbital.reshape(rows, n_aux * n_occ)
        me = lax.axis_index("grp")
        pos = jnp.asarray(pos_of)[me]
        ring_c = jnp.asarray(ring_arr)

        def start_of(off):
            return ring_c[(pos + off) % n] * rows

        radius = n // 4
        held = {0: orbital}
        fwd = orbital
        bwd = orbital
        for k in range(1, radius + 1):
            fwd = lax.ppermute(fwd, "grp", shifted(1))
            held[-k] = fwd
            bwd = lax.ppermute(bwd, "grp", shifted(-1))
            held[k] = bwd

        def prod(xo, yo):
            return jnp.dot(held[xo], held[yo].T, preferred_element_type=jnp.float32)

        local = []
        outgoing = {}
        for d in range(n // 2 + 1):
            xo = -((d + 1) // 2)
            yo = xo + d
            blk = prod(xo, yo)
            s = d // 2
            if s == 0:
                local.append((-d, blk))
            else:
                outgoing.setdefault(s, []).append((-d, blk))
            if 0 < d < n // 2:
                outgoing.setdefault(xo, []).append((d, blk.T))
        placed = list(local)
        for s, items in sorted(outgoing.items()):
            stack = jnp.stack([b for _, b in items])
            got = lax.ppermute(stack, "grp", shifted(s))
            placed += [(off, got[i]) for i, (off, _) in enumerate(items)]
        term = jnp.zeros((n * rows, rows), jnp.float32)
        for off, blk in placed:
            term = lax.dynamic_update_slice_in_dim(term, blk, start_of(off), axis=0)
        return scatter_sum(term)

    return body


def solution(mesh):
    return jax.shard_map(
        make_body(ring_order(mesh)),
        mesh=mesh,
        in_specs=(P("rep", "grp", None, None, None), P("rep", None, None), P(), P(), P(), P()),
        out_specs=P("rep", "grp"),
        check_vma=False,
    )
```

```python
import jax
import jax.numpy as jnp
import numpy as np
from jax import lax
from jax.sharding import PartitionSpec as P

NB = 64


def snake(a_size, b_size):
    if a_size % 2:
        return [(a, b) for b, a in snake(b_size, a_size)]
    if b_size == 1:
        return [(a, 0) for a in range(a_size)]
    path = []
    for a in range(a_size):
        cols = range(b_size) if a == 0 else (range(1, b_size) if a % 2 == 0 else range(b_size - 1, 0, -1))
        path += [(a, b) for b in cols]
    path += [(a, 0) for a in range(a_size - 1, 0, -1)]
    return path


def ring_order(mesh):
    n = mesh.shape["grp"]
    try:
        devs = np.asarray(mesh.devices).reshape(n, -1)[:, 0]
        coords = [tuple(d.coords) for d in devs]
    except (AttributeError, TypeError):
        return list(range(n))
    varying = [i for i in range(len(coords[0])) if len({c[i] for c in coords}) > 1]
    if len(varying) == 1:
        key = sorted(range(n), key=lambda g: coords[g][varying[0]])
        return key
    if len(varying) != 2:
        return list(range(n))
    i, j = varying
    avals = sorted({c[i] for c in coords})
    bvals = sorted({c[j] for c in coords})
    where = {(avals.index(c[i]), bvals.index(c[j])): g for g, c in enumerate(coords)}
    if len(where) != n:
        return list(range(n))
    return [where[p] for p in snake(len(avals), len(bvals))]


def scatter_sum(term):
    n_rep = lax.axis_size("rep")
    if n_rep & (n_rep - 1):
        return lax.psum_scatter(term, "rep", scatter_dimension=0, tiled=True)
    me = lax.axis_index("rep")
    bits = n_rep.bit_length() - 1
    per = term.shape[0] // n_rep
    buf = term.reshape((2,) * bits + (per,) + term.shape[1:])
    for b in range(bits):
        d = 1 << b
        axis = buf.ndim - 3
        mine = (me // d) % 2
        keep = lax.dynamic_index_in_dim(buf, mine, axis=axis, keepdims=False)
        send = lax.dynamic_index_in_dim(buf, 1 - mine, axis=axis, keepdims=False)
        got = lax.ppermute(send, "rep", [(i, i ^ d) for i in range(n_rep)])
        buf = keep + got
    return buf.reshape(per, term.shape[1])


def make_body(ring):
    n = len(ring)
    pos_of = np.zeros(n, np.int32)
    for p, g in enumerate(ring):
        pos_of[g] = p
    ring_arr = np.asarray(ring, np.int32)

    def shifted(s):
        return [(ring[p], ring[(p + s) % n]) for p in range(n)]

    def body(three_center, metric, occupied, nu_list, nu_count, block_size):
        n_mu, knu = nu_list.shape
        n_occ = occupied.shape[1]
        aux_dev = three_center.shape[1]
        lanes = jnp.arange(NB, dtype=jnp.int32)
        row_live = lanes[None, :] < block_size[:, None]
        col_live = lanes[None, None, :] < block_size[nu_list][:, :, None]
        slot_live = jnp.arange(knu, dtype=jnp.int32)[None, :] < nu_count[:, None]
        keep = col_live & slot_live[:, :, None]
        picked = occupied.reshape(n_mu, NB, n_occ)[nu_list]
        picked = jnp.where(keep[..., None], picked, jnp.zeros((), jnp.bfloat16))
        pair = 2
        blank = jnp.zeros_like(picked)
        weight = jnp.concatenate(
            [jnp.concatenate([picked, blank], axis=-1), jnp.concatenate([blank, picked], axis=-1)], axis=-2
        )
        tiles = NB // pair
        tc = jnp.swapaxes(three_center[0], 1, 2).reshape(aux_dev, knu, n_mu, tiles, pair * NB)
        half = jnp.einsum("qkmtl,mklc->qmtc", tc, weight, preferred_element_type=jnp.float32)
        half = half.reshape(aux_dev, n_mu, NB, n_occ)
        half = jnp.where(row_live[None, :, :, None], half, 0.0).astype(jnp.bfloat16)
        half = half.reshape(aux_dev, n_mu, NB * n_occ)
        me = lax.axis_index("grp")
        pos = jnp.asarray(pos_of)[me]
        ring_c = jnp.asarray(ring_arr)
        mu_dev = n_mu // n
        pieces = []
        for s in range(n):
            dest = ring_c[(pos + s) % n]
            piece = lax.dynamic_slice_in_dim(half, dest * mu_dev, mu_dev, axis=1)
            if s:
                piece = lax.ppermute(piece, "grp", shifted(s))
            pieces.append(piece)
        stacked = jnp.stack(pieces).reshape(n, aux_dev, mu_dev, NB, n_occ)
        srcs = ring_c[(pos - jnp.arange(n, dtype=jnp.int32)) % n]
        cols = (srcs[:, None] * aux_dev + jnp.arange(aux_dev, dtype=jnp.int32)[None, :]).reshape(-1)
        factor = jnp.take(metric[0], cols, axis=1).reshape(-1, n, aux_dev)
        orbital = jnp.einsum(
            "psq,sqmai->mapi", factor, stacked, preferred_element_type=jnp.float32
        ).astype(jnp.bfloat16)
        n_aux = n * aux_dev
        rows = mu_dev * NB
        orbital = orbital.reshape(rows, n_aux * n_occ)
        def start_of(off):
            return ring_c[(pos + off) % n] * rows

        radius = n // 4
        held = {0: orbital}
        fwd = orbital
        bwd = orbital
        for k in range(1, radius + 1):
            fwd = lax.ppermute(fwd, "grp", shifted(1))
            held[-k] = fwd
            bwd = lax.ppermute(bwd, "grp", shifted(-1))
            held[k] = bwd

        def prod(xo, yo):
            return jnp.dot(held[xo], held[yo].T, preferred_element_type=jnp.float32)

        local = []
        outgoing = {}
        for d in range(n // 2 + 1):
            xo = -((d + 1) // 2)
            yo = xo + d
            blk = prod(xo, yo)
            s = d // 2
            if s == 0:
                local.append((-d, blk))
            else:
                outgoing.setdefault(s, []).append((-d, blk))
            if 0 < d < n // 2:
                outgoing.setdefault(xo, []).append((d, blk.T))
        placed = list(local)
        for s, items in sorted(outgoing.items()):
            stack = jnp.stack([b for _, b in items])
            got = lax.ppermute(stack, "grp", shifted(s))
            placed += [(off, got[i]) for i, (off, _) in enumerate(items)]
        term = jnp.zeros((n * rows, rows), jnp.float32)
        for off, blk in placed:
            term = lax.dynamic_update_slice_in_dim(term, blk, start_of(off), axis=0)
        return scatter_sum(term)

    return body


def solution(mesh):
    return jax.shard_map(
        make_body(ring_order(mesh)),
        mesh=mesh,
        in_specs=(P("rep", "grp", None, None, None), P("rep", None, None), P(), P(), P(), P()),
        out_specs=P("rep", "grp"),
        check_vma=False,
    )
```

```python
import jax
import jax.numpy as jnp
import numpy as np
from jax import lax
from jax.sharding import PartitionSpec as P

NB = 64


def snake(a_size, b_size):
    if a_size % 2:
        return [(a, b) for b, a in snake(b_size, a_size)]
    if b_size == 1:
        return [(a, 0) for a in range(a_size)]
    path = []
    for a in range(a_size):
        cols = range(b_size) if a == 0 else (range(1, b_size) if a % 2 == 0 else range(b_size - 1, 0, -1))
        path += [(a, b) for b in cols]
    path += [(a, 0) for a in range(a_size - 1, 0, -1)]
    return path


def ring_order(mesh):
    n = mesh.shape["grp"]
    try:
        devs = np.asarray(mesh.devices).reshape(n, -1)[:, 0]
        coords = [tuple(d.coords) for d in devs]
    except (AttributeError, TypeError):
        return list(range(n))
    varying = [i for i in range(len(coords[0])) if len({c[i] for c in coords}) > 1]
    if len(varying) == 1:
        key = sorted(range(n), key=lambda g: coords[g][varying[0]])
        return key
    if len(varying) != 2:
        return list(range(n))
    i, j = varying
    avals = sorted({c[i] for c in coords})
    bvals = sorted({c[j] for c in coords})
    where = {(avals.index(c[i]), bvals.index(c[j])): g for g, c in enumerate(coords)}
    if len(where) != n:
        return list(range(n))
    return [where[p] for p in snake(len(avals), len(bvals))]


def scatter_sum(term):
    n_rep = lax.axis_size("rep")
    if n_rep & (n_rep - 1):
        return lax.psum_scatter(term, "rep", scatter_dimension=0, tiled=True)
    me = lax.axis_index("rep")
    bits = n_rep.bit_length() - 1
    per = term.shape[0] // n_rep
    buf = term.reshape((2,) * bits + (per,) + term.shape[1:])
    for b in range(bits):
        d = 1 << b
        axis = buf.ndim - 3
        mine = (me // d) % 2
        keep = lax.dynamic_index_in_dim(buf, mine, axis=axis, keepdims=False)
        send = lax.dynamic_index_in_dim(buf, 1 - mine, axis=axis, keepdims=False)
        got = lax.ppermute(send, "rep", [(i, i ^ d) for i in range(n_rep)])
        buf = keep + got
    return buf.reshape(per, term.shape[1])


def make_body(ring):
    n = len(ring)
    pos_of = np.zeros(n, np.int32)
    for p, g in enumerate(ring):
        pos_of[g] = p
    ring_arr = np.asarray(ring, np.int32)

    def shifted(s):
        return [(ring[p], ring[(p + s) % n]) for p in range(n)]

    def body(three_center, metric, occupied, nu_list, nu_count, block_size):
        n_mu, knu = nu_list.shape
        n_occ = occupied.shape[1]
        aux_dev = three_center.shape[1]
        lanes = jnp.arange(NB, dtype=jnp.int32)
        row_live = lanes[None, :] < block_size[:, None]
        col_live = lanes[None, None, :] < block_size[nu_list][:, :, None]
        slot_live = jnp.arange(knu, dtype=jnp.int32)[None, :] < nu_count[:, None]
        keep = col_live & slot_live[:, :, None]
        picked = occupied.reshape(n_mu, NB, n_occ)[nu_list]
        picked = jnp.where(keep[..., None], picked, jnp.zeros((), jnp.bfloat16))
        pair = 2
        blank = jnp.zeros_like(picked)
        weight = jnp.concatenate(
            [jnp.concatenate([picked, blank], axis=-1), jnp.concatenate([blank, picked], axis=-1)], axis=-2
        )
        tiles = NB // pair
        tc = jnp.swapaxes(three_center[0], 1, 2).reshape(aux_dev, knu, n_mu, tiles, pair * NB)
        half = jnp.einsum("qkmtl,mklc->qmtc", tc, weight, preferred_element_type=jnp.float32)
        half = half.reshape(aux_dev, n_mu, NB, n_occ)
        half = jnp.where(row_live[None, :, :, None], half, 0.0).astype(jnp.bfloat16)
        half = half.reshape(aux_dev, n_mu, NB * n_occ)
        regrouped = lax.all_to_all(half, "grp", split_axis=1, concat_axis=0, tiled=True)
        n_aux = regrouped.shape[0]
        mu_dev = regrouped.shape[1]
        mixed = jnp.dot(metric[0], regrouped.reshape(n_aux, -1), preferred_element_type=jnp.float32)
        mixed = mixed.astype(jnp.bfloat16).reshape(n_aux, mu_dev, NB, n_occ)
        orbital = jnp.transpose(mixed, (1, 2, 0, 3))
        rows = mu_dev * NB
        orbital = orbital.reshape(rows, n_aux * n_occ)
        me = lax.axis_index("grp")
        pos = jnp.asarray(pos_of)[me]
        ring_c = jnp.asarray(ring_arr)

        def start_of(off):
            return ring_c[(pos + off) % n] * rows

        radius = n // 4
        held = {0: orbital}
        fwd = orbital
        bwd = orbital
        for k in range(1, radius + 1):
            fwd = lax.ppermute(fwd, "grp", shifted(1))
            held[-k] = fwd
            bwd = lax.ppermute(bwd, "grp", shifted(-1))
            held[k] = bwd

        def prod(xo, yo):
            return jnp.dot(held[xo], held[yo].T, preferred_element_type=jnp.float32)

        local = []
        outgoing = {}
        for d in range(n // 2 + 1):
            xo = -((d + 1) // 2)
            yo = xo + d
            blk = prod(xo, yo)
            s = d // 2
            if s == 0:
                local.append((-d, blk))
            else:
                outgoing.setdefault(s, []).append((-d, blk))
            if 0 < d < n // 2:
                outgoing.setdefault(xo, []).append((d, blk.T))
        placed = list(local)
        for s, items in sorted(outgoing.items()):
            stack = jnp.stack([b for _, b in items])
            got = lax.ppermute(stack, "grp", shifted(s))
            placed += [(off, got[i]) for i, (off, _) in enumerate(items)]
        term = jnp.zeros((n * rows, rows), jnp.float32)
        for off, blk in placed:
            term = lax.dynamic_update_slice_in_dim(term, blk, start_of(off), axis=0)
        return scatter_sum(term)

    return body


def solution(mesh):
    return jax.shard_map(
        make_body(ring_order(mesh)),
        mesh=mesh,
        in_specs=(P("rep", "grp", None, None, None), P("rep", None, None), P(), P(), P(), P()),
        out_specs=P("rep", "grp"),
        check_vma=False,
    )
```

```python
import jax
import jax.numpy as jnp
import numpy as np
from jax import lax
from jax.sharding import PartitionSpec as P

NB = 64


def snake(a_size, b_size):
    if a_size % 2:
        return [(a, b) for b, a in snake(b_size, a_size)]
    if b_size == 1:
        return [(a, 0) for a in range(a_size)]
    path = []
    for a in range(a_size):
        cols = range(b_size) if a == 0 else (range(1, b_size) if a % 2 == 0 else range(b_size - 1, 0, -1))
        path += [(a, b) for b in cols]
    path += [(a, 0) for a in range(a_size - 1, 0, -1)]
    return path


def ring_order(mesh):
    n = mesh.shape["grp"]
    try:
        devs = np.asarray(mesh.devices).reshape(n, -1)[:, 0]
        coords = [tuple(d.coords) for d in devs]
    except (AttributeError, TypeError):
        return list(range(n))
    varying = [i for i in range(len(coords[0])) if len({c[i] for c in coords}) > 1]
    if len(varying) == 1:
        key = sorted(range(n), key=lambda g: coords[g][varying[0]])
        return key
    if len(varying) != 2:
        return list(range(n))
    i, j = varying
    avals = sorted({c[i] for c in coords})
    bvals = sorted({c[j] for c in coords})
    where = {(avals.index(c[i]), bvals.index(c[j])): g for g, c in enumerate(coords)}
    if len(where) != n:
        return list(range(n))
    return [where[p] for p in snake(len(avals), len(bvals))]


def scatter_sum(term):
    n_rep = lax.axis_size("rep")
    if n_rep & (n_rep - 1):
        return lax.psum_scatter(term, "rep", scatter_dimension=0, tiled=True)
    me = lax.axis_index("rep")
    bits = n_rep.bit_length() - 1
    per = term.shape[0] // n_rep
    buf = term.reshape((2,) * bits + (per,) + term.shape[1:])
    for b in range(bits):
        d = 1 << b
        axis = buf.ndim - 3
        mine = (me // d) % 2
        keep = lax.dynamic_index_in_dim(buf, mine, axis=axis, keepdims=False)
        send = lax.dynamic_index_in_dim(buf, 1 - mine, axis=axis, keepdims=False)
        got = lax.ppermute(send, "rep", [(i, i ^ d) for i in range(n_rep)])
        buf = keep + got
    return buf.reshape(per, term.shape[1])


def make_body(ring):
    n = len(ring)
    pos_of = np.zeros(n, np.int32)
    for p, g in enumerate(ring):
        pos_of[g] = p
    ring_arr = np.asarray(ring, np.int32)

    def shifted(s):
        return [(ring[p], ring[(p + s) % n]) for p in range(n)]

    def body(three_center, metric, occupied, nu_list, nu_count, block_size):
        n_mu, knu = nu_list.shape
        n_occ = occupied.shape[1]
        aux_dev = three_center.shape[1]
        lanes = jnp.arange(NB, dtype=jnp.int32)
        row_live = lanes[None, :] < block_size[:, None]
        col_live = lanes[None, None, :] < block_size[nu_list][:, :, None]
        slot_live = jnp.arange(knu, dtype=jnp.int32)[None, :] < nu_count[:, None]
        keep = col_live & slot_live[:, :, None]
        picked = occupied.reshape(n_mu, NB, n_occ)[nu_list]
        picked = jnp.where(keep[..., None], picked, jnp.zeros((), jnp.bfloat16))
        pair = 2
        blank = jnp.zeros_like(picked)
        weight = jnp.concatenate(
            [jnp.concatenate([picked, blank], axis=-1), jnp.concatenate([blank, picked], axis=-1)], axis=-2
        )
        tiles = NB // pair
        tc = jnp.swapaxes(three_center[0], 1, 2).reshape(aux_dev, knu, n_mu, tiles, pair * NB)
        half = jnp.einsum("qkmtl,mklc->qmtc", tc, weight, preferred_element_type=jnp.float32)
        half = half.reshape(aux_dev, n_mu, NB, n_occ)
        half = jnp.where(row_live[None, :, :, None], half, 0.0).astype(jnp.bfloat16)
        half = half.reshape(aux_dev, n_mu, NB * n_occ)
        regrouped = lax.all_to_all(half, "grp", split_axis=1, concat_axis=0, tiled=True)
        n_aux = regrouped.shape[0]
        mu_dev = regrouped.shape[1]
        orbital = lax.dot_general(
            regrouped.reshape(n_aux, mu_dev * NB, n_occ), metric[0], (((0,), (1,)), ((), ())),
            preferred_element_type=jnp.float32,
        ).astype(jnp.bfloat16)
        rows = mu_dev * NB
        orbital = orbital.reshape(rows, n_aux * n_occ)
        me = lax.axis_index("grp")
        pos = jnp.asarray(pos_of)[me]
        ring_c = jnp.asarray(ring_arr)

        def start_of(off):
            return ring_c[(pos + off) % n] * rows

        radius = n // 4
        held = {0: orbital}
        fwd = orbital
        bwd = orbital
        for k in range(1, radius + 1):
            fwd = lax.ppermute(fwd, "grp", shifted(1))
            held[-k] = fwd
            bwd = lax.ppermute(bwd, "grp", shifted(-1))
            held[k] = bwd

        def prod(xo, yo):
            return jnp.dot(held[xo], held[yo].T, preferred_element_type=jnp.float32)

        local = []
        outgoing = {}
        for d in range(n // 2 + 1):
            xo = -((d + 1) // 2)
            yo = xo + d
            blk = prod(xo, yo)
            s = d // 2
            if s == 0:
                local.append((-d, blk))
            else:
                outgoing.setdefault(s, []).append((-d, blk))
            if 0 < d < n // 2:
                outgoing.setdefault(xo, []).append((d, blk.T))
        placed = list(local)
        for s, items in sorted(outgoing.items()):
            stack = jnp.stack([b for _, b in items])
            got = lax.ppermute(stack, "grp", shifted(s))
            placed += [(off, got[i]) for i, (off, _) in enumerate(items)]
        term = jnp.zeros((n * rows, rows), jnp.float32)
        for off, blk in placed:
            term = lax.dynamic_update_slice_in_dim(term, blk, start_of(off), axis=0)
        return scatter_sum(term)

    return body


def solution(mesh):
    return jax.shard_map(
        make_body(ring_order(mesh)),
        mesh=mesh,
        in_specs=(P("rep", "grp", None, None, None), P("rep", None, None), P(), P(), P(), P()),
        out_specs=P("rep", "grp"),
        check_vma=False,
    )
```

```python
import jax
import jax.numpy as jnp
import numpy as np
from jax import lax
from jax.sharding import PartitionSpec as P

NB = 64


def snake(a_size, b_size):
    if a_size % 2:
        return [(a, b) for b, a in snake(b_size, a_size)]
    if b_size == 1:
        return [(a, 0) for a in range(a_size)]
    path = []
    for a in range(a_size):
        cols = range(b_size) if a == 0 else (range(1, b_size) if a % 2 == 0 else range(b_size - 1, 0, -1))
        path += [(a, b) for b in cols]
    path += [(a, 0) for a in range(a_size - 1, 0, -1)]
    return path


def ring_order(mesh):
    n = mesh.shape["grp"]
    try:
        devs = np.asarray(mesh.devices).reshape(n, -1)[:, 0]
        coords = [tuple(d.coords) for d in devs]
    except (AttributeError, TypeError):
        return list(range(n))
    varying = [i for i in range(len(coords[0])) if len({c[i] for c in coords}) > 1]
    if len(varying) == 1:
        key = sorted(range(n), key=lambda g: coords[g][varying[0]])
        return key
    if len(varying) != 2:
        return list(range(n))
    i, j = varying
    avals = sorted({c[i] for c in coords})
    bvals = sorted({c[j] for c in coords})
    where = {(avals.index(c[i]), bvals.index(c[j])): g for g, c in enumerate(coords)}
    if len(where) != n:
        return list(range(n))
    return [where[p] for p in snake(len(avals), len(bvals))]


def scatter_sum(term):
    n_rep = lax.axis_size("rep")
    if n_rep & (n_rep - 1):
        return lax.psum_scatter(term, "rep", scatter_dimension=0, tiled=True)
    me = lax.axis_index("rep")
    bits = n_rep.bit_length() - 1
    per = term.shape[0] // n_rep
    buf = term.reshape((2,) * bits + (per,) + term.shape[1:])
    for b in range(bits):
        d = 1 << b
        axis = buf.ndim - 3
        mine = (me // d) % 2
        keep = lax.dynamic_index_in_dim(buf, mine, axis=axis, keepdims=False)
        send = lax.dynamic_index_in_dim(buf, 1 - mine, axis=axis, keepdims=False)
        got = lax.ppermute(send, "rep", [(i, i ^ d) for i in range(n_rep)])
        buf = keep + got
    return buf.reshape(per, term.shape[1])


def make_body(ring):
    n = len(ring)
    pos_of = np.zeros(n, np.int32)
    for p, g in enumerate(ring):
        pos_of[g] = p
    ring_arr = np.asarray(ring, np.int32)

    def shifted(s):
        return [(ring[p], ring[(p + s) % n]) for p in range(n)]

    def body(three_center, metric, occupied, nu_list, nu_count, block_size):
        n_mu, knu = nu_list.shape
        n_occ = occupied.shape[1]
        aux_dev = three_center.shape[1]
        lanes = jnp.arange(NB, dtype=jnp.int32)
        row_live = lanes[None, :] < block_size[:, None]
        col_live = lanes[None, None, :] < block_size[nu_list][:, :, None]
        slot_live = jnp.arange(knu, dtype=jnp.int32)[None, :] < nu_count[:, None]
        keep = col_live & slot_live[:, :, None]
        picked = occupied.reshape(n_mu, NB, n_occ)[nu_list]
        picked = jnp.where(keep[..., None], picked, jnp.zeros((), jnp.bfloat16))
        pair = 4
        blank = jnp.zeros_like(picked)
        weight = jnp.concatenate(
            [jnp.concatenate([picked if j == r else blank for j in range(pair)], axis=-1) for r in range(pair)],
            axis=-2,
        )
        tiles = NB // pair
        tc = jnp.swapaxes(three_center[0], 1, 2).reshape(aux_dev, knu, n_mu, tiles, pair * NB)
        half = jnp.einsum("qkmtl,mklc->qmtc", tc, weight, preferred_element_type=jnp.float32)
        half = half.reshape(aux_dev, n_mu, NB, n_occ)
        half = jnp.where(row_live[None, :, :, None], half, 0.0).astype(jnp.bfloat16)
        half = half.reshape(aux_dev, n_mu, NB * n_occ)
        regrouped = lax.all_to_all(half, "grp", split_axis=1, concat_axis=0, tiled=True)
        n_aux = regrouped.shape[0]
        mu_dev = regrouped.shape[1]
        mixed = jnp.dot(metric[0], regrouped.reshape(n_aux, -1), preferred_element_type=jnp.float32)
        mixed = mixed.astype(jnp.bfloat16).reshape(n_aux, mu_dev, NB, n_occ)
        orbital = jnp.transpose(mixed, (1, 2, 0, 3))
        rows = mu_dev * NB
        orbital = orbital.reshape(rows, n_aux * n_occ)
        me = lax.axis_index("grp")
        pos = jnp.asarray(pos_of)[me]
        ring_c = jnp.asarray(ring_arr)

        def start_of(off):
            return ring_c[(pos + off) % n] * rows

        radius = n // 4
        held = {0: orbital}
        fwd = orbital
        bwd = orbital
        for k in range(1, radius + 1):
            fwd = lax.ppermute(fwd, "grp", shifted(1))
            held[-k] = fwd
            bwd = lax.ppermute(bwd, "grp", shifted(-1))
            held[k] = bwd

        def prod(xo, yo):
            return jnp.dot(held[xo], held[yo].T, preferred_element_type=jnp.float32)

        local = []
        outgoing = {}
        for d in range(n // 2 + 1):
            xo = -((d + 1) // 2)
            yo = xo + d
            blk = prod(xo, yo)
            s = d // 2
            if s == 0:
                local.append((-d, blk))
            else:
                outgoing.setdefault(s, []).append((-d, blk))
            if 0 < d < n // 2:
                outgoing.setdefault(xo, []).append((d, blk.T))
        placed = list(local)
        for s, items in sorted(outgoing.items()):
            stack = jnp.stack([b for _, b in items])
            got = lax.ppermute(stack, "grp", shifted(s))
            placed += [(off, got[i]) for i, (off, _) in enumerate(items)]
        term = jnp.zeros((n * rows, rows), jnp.float32)
        for off, blk in placed:
            term = lax.dynamic_update_slice_in_dim(term, blk, start_of(off), axis=0)
        return scatter_sum(term)

    return body


def solution(mesh):
    return jax.shard_map(
        make_body(ring_order(mesh)),
        mesh=mesh,
        in_specs=(P("rep", "grp", None, None, None), P("rep", None, None), P(), P(), P(), P()),
        out_specs=P("rep", "grp"),
        check_vma=False,
    )
```

```python
import jax
import jax.numpy as jnp
import numpy as np
from jax import lax
from jax.sharding import PartitionSpec as P

NB = 64


def snake(a_size, b_size):
    if a_size % 2:
        return [(a, b) for b, a in snake(b_size, a_size)]
    if b_size == 1:
        return [(a, 0) for a in range(a_size)]
    path = []
    for a in range(a_size):
        cols = range(b_size) if a == 0 else (range(1, b_size) if a % 2 == 0 else range(b_size - 1, 0, -1))
        path += [(a, b) for b in cols]
    path += [(a, 0) for a in range(a_size - 1, 0, -1)]
    return path


def ring_order(mesh):
    n = mesh.shape["grp"]
    try:
        devs = np.asarray(mesh.devices).reshape(n, -1)[:, 0]
        coords = [tuple(d.coords) for d in devs]
    except (AttributeError, TypeError):
        return list(range(n))
    varying = [i for i in range(len(coords[0])) if len({c[i] for c in coords}) > 1]
    if len(varying) == 1:
        key = sorted(range(n), key=lambda g: coords[g][varying[0]])
        return key
    if len(varying) != 2:
        return list(range(n))
    i, j = varying
    avals = sorted({c[i] for c in coords})
    bvals = sorted({c[j] for c in coords})
    where = {(avals.index(c[i]), bvals.index(c[j])): g for g, c in enumerate(coords)}
    if len(where) != n:
        return list(range(n))
    return [where[p] for p in snake(len(avals), len(bvals))]


def scatter_sum(term):
    n_rep = lax.axis_size("rep")
    if n_rep & (n_rep - 1):
        return lax.psum_scatter(term, "rep", scatter_dimension=0, tiled=True)
    me = lax.axis_index("rep")
    bits = n_rep.bit_length() - 1
    per = term.shape[0] // n_rep
    buf = term.reshape((2,) * bits + (per,) + term.shape[1:])
    for b in range(bits):
        d = 1 << b
        axis = buf.ndim - 3
        mine = (me // d) % 2
        keep = lax.dynamic_index_in_dim(buf, mine, axis=axis, keepdims=False)
        send = lax.dynamic_index_in_dim(buf, 1 - mine, axis=axis, keepdims=False)
        got = lax.ppermute(send, "rep", [(i, i ^ d) for i in range(n_rep)])
        buf = keep + got
    return buf.reshape(per, term.shape[1])


def make_body(ring):
    n = len(ring)
    pos_of = np.zeros(n, np.int32)
    for p, g in enumerate(ring):
        pos_of[g] = p
    ring_arr = np.asarray(ring, np.int32)

    def shifted(s):
        return [(ring[p], ring[(p + s) % n]) for p in range(n)]

    def body(three_center, metric, occupied, nu_list, nu_count, block_size):
        n_mu, knu = nu_list.shape
        n_occ = occupied.shape[1]
        aux_dev = three_center.shape[1]
        lanes = jnp.arange(NB, dtype=jnp.int32)
        row_live = lanes[None, :] < block_size[:, None]
        col_live = lanes[None, None, :] < block_size[nu_list][:, :, None]
        slot_live = jnp.arange(knu, dtype=jnp.int32)[None, :] < nu_count[:, None]
        keep = col_live & slot_live[:, :, None]
        picked = occupied.reshape(n_mu, NB, n_occ)[nu_list]
        picked = jnp.where(keep[..., None], picked, jnp.zeros((), jnp.bfloat16))
        me = lax.axis_index("grp")
        pos = jnp.asarray(pos_of)[me]
        ring_c = jnp.asarray(ring_arr)
        pair = 2
        tiles = NB // pair
        tc = jnp.swapaxes(three_center[0], 1, 2).reshape(aux_dev, knu, n_mu, tiles, pair * NB)
        n_split = 2 if n_occ % 2 == 0 else 1
        occ_c = n_occ // n_split
        radius = n // 4
        helds = []
        for h in range(n_split):
            part = picked[..., h * occ_c:(h + 1) * occ_c]
            blank = jnp.zeros_like(part)
            weight = jnp.concatenate(
                [jnp.concatenate([part, blank], axis=-1), jnp.concatenate([blank, part], axis=-1)], axis=-2
            )
            half = jnp.einsum("qkmtl,mklc->qmtc", tc, weight, preferred_element_type=jnp.float32)
            half = half.reshape(aux_dev, n_mu, NB, occ_c)
            half = jnp.where(row_live[None, :, :, None], half, 0.0).astype(jnp.bfloat16)
            half = half.reshape(aux_dev, n_mu, NB * occ_c)
            regrouped = lax.all_to_all(half, "grp", split_axis=1, concat_axis=0, tiled=True)
            n_aux = regrouped.shape[0]
            mu_dev = regrouped.shape[1]
            mixed = jnp.dot(metric[0], regrouped.reshape(n_aux, -1), preferred_element_type=jnp.float32)
            mixed = mixed.astype(jnp.bfloat16).reshape(n_aux, mu_dev, NB, occ_c)
            orbital = jnp.transpose(mixed, (1, 2, 0, 3))
            rows = mu_dev * NB
            orbital = orbital.reshape(rows, n_aux * occ_c)
            held = {0: orbital}
            fwd = orbital
            bwd = orbital
            for k in range(1, radius + 1):
                fwd = lax.ppermute(fwd, "grp", shifted(1))
                held[-k] = fwd
                bwd = lax.ppermute(bwd, "grp", shifted(-1))
                held[k] = bwd
            helds.append(held)

        def start_of(off):
            return ring_c[(pos + off) % n] * rows

        def prod(xo, yo):
            out = None
            for held in helds:
                one = jnp.dot(held[xo], held[yo].T, preferred_element_type=jnp.float32)
                out = one if out is None else out + one
            return out

        local = []
        outgoing = {}
        for d in range(n // 2 + 1):
            xo = -((d + 1) // 2)
            yo = xo + d
            blk = prod(xo, yo)
            s = d // 2
            if s == 0:
                local.append((-d, blk))
            else:
                outgoing.setdefault(s, []).append((-d, blk))
            if 0 < d < n // 2:
                outgoing.setdefault(xo, []).append((d, blk.T))
        placed = list(local)
        for s, items in sorted(outgoing.items()):
            stack = jnp.stack([b for _, b in items])
            got = lax.ppermute(stack, "grp", shifted(s))
            placed += [(off, got[i]) for i, (off, _) in enumerate(items)]
        term = jnp.zeros((n * rows, rows), jnp.float32)
        for off, blk in placed:
            term = lax.dynamic_update_slice_in_dim(term, blk, start_of(off), axis=0)
        return scatter_sum(term)

    return body


def solution(mesh):
    return jax.shard_map(
        make_body(ring_order(mesh)),
        mesh=mesh,
        in_specs=(P("rep", "grp", None, None, None), P("rep", None, None), P(), P(), P(), P()),
        out_specs=P("rep", "grp"),
        check_vma=False,
    )
```

```python
import jax
import jax.numpy as jnp
import numpy as np
from jax import lax
from jax.sharding import PartitionSpec as P

NB = 64


def snake(a_size, b_size):
    if a_size % 2:
        return [(a, b) for b, a in snake(b_size, a_size)]
    if b_size == 1:
        return [(a, 0) for a in range(a_size)]
    path = []
    for a in range(a_size):
        cols = range(b_size) if a == 0 else (range(1, b_size) if a % 2 == 0 else range(b_size - 1, 0, -1))
        path += [(a, b) for b in cols]
    path += [(a, 0) for a in range(a_size - 1, 0, -1)]
    return path


def ring_order(mesh):
    n = mesh.shape["grp"]
    try:
        devs = np.asarray(mesh.devices).reshape(n, -1)[:, 0]
        coords = [tuple(d.coords) for d in devs]
    except (AttributeError, TypeError):
        return list(range(n))
    varying = [i for i in range(len(coords[0])) if len({c[i] for c in coords}) > 1]
    if len(varying) == 1:
        key = sorted(range(n), key=lambda g: coords[g][varying[0]])
        return key
    if len(varying) != 2:
        return list(range(n))
    i, j = varying
    avals = sorted({c[i] for c in coords})
    bvals = sorted({c[j] for c in coords})
    where = {(avals.index(c[i]), bvals.index(c[j])): g for g, c in enumerate(coords)}
    if len(where) != n:
        return list(range(n))
    return [where[p] for p in snake(len(avals), len(bvals))]


def scatter_sum(term):
    n_rep = lax.axis_size("rep")
    if n_rep & (n_rep - 1):
        return lax.psum_scatter(term, "rep", scatter_dimension=0, tiled=True)
    me = lax.axis_index("rep")
    bits = n_rep.bit_length() - 1
    per = term.shape[0] // n_rep
    buf = term.reshape((2,) * bits + (per,) + term.shape[1:])
    for b in range(bits):
        d = 1 << b
        axis = buf.ndim - 3
        mine = (me // d) % 2
        keep = lax.dynamic_index_in_dim(buf, mine, axis=axis, keepdims=False)
        send = lax.dynamic_index_in_dim(buf, 1 - mine, axis=axis, keepdims=False)
        got = lax.ppermute(send, "rep", [(i, i ^ d) for i in range(n_rep)])
        buf = keep + got
    return buf.reshape(per, term.shape[1])


def make_body(ring):
    n = len(ring)
    pos_of = np.zeros(n, np.int32)
    for p, g in enumerate(ring):
        pos_of[g] = p
    ring_arr = np.asarray(ring, np.int32)

    def shifted(s):
        return [(ring[p], ring[(p + s) % n]) for p in range(n)]

    def body(three_center, metric, occupied, nu_list, nu_count, block_size):
        n_mu, knu = nu_list.shape
        n_occ = occupied.shape[1]
        aux_dev = three_center.shape[1]
        lanes = jnp.arange(NB, dtype=jnp.int32)
        row_live = lanes[None, :] < block_size[:, None]
        col_live = lanes[None, None, :] < block_size[nu_list][:, :, None]
        slot_live = jnp.arange(knu, dtype=jnp.int32)[None, :] < nu_count[:, None]
        keep = col_live & slot_live[:, :, None]
        picked = occupied.reshape(n_mu, NB, n_occ)[nu_list]
        picked = jnp.where(keep[..., None], picked, jnp.zeros((), jnp.bfloat16))
        me = lax.axis_index("grp")
        pos = jnp.asarray(pos_of)[me]
        ring_c = jnp.asarray(ring_arr)
        pair = 2
        tiles = NB // pair
        tc = jnp.swapaxes(three_center[0], 1, 2).reshape(aux_dev, knu, n_mu, tiles, pair * NB)
        n_split = 2 if n_occ % 2 == 0 else 1
        occ_c = n_occ // n_split
        radius = n // 4
        helds = []
        pieces = picked.reshape(n_mu, knu, NB, n_split, occ_c)
        blank = jnp.zeros_like(pieces)
        weight = jnp.concatenate(
            [jnp.concatenate([pieces, blank], axis=-1), jnp.concatenate([blank, pieces], axis=-1)], axis=-3
        )
        whole = jnp.einsum("qkmtl,mklhc->qmthc", tc, weight, preferred_element_type=jnp.float32)
        whole = whole.reshape(aux_dev, n_mu, tiles, n_split, pair, occ_c)
        whole = jnp.where(row_live.reshape(1, n_mu, tiles, 1, pair, 1), whole, 0.0).astype(jnp.bfloat16)
        for h in range(n_split):
            half = whole[:, :, :, h].reshape(aux_dev, n_mu, NB * occ_c)
            regrouped = lax.all_to_all(half, "grp", split_axis=1, concat_axis=0, tiled=True)
            n_aux = regrouped.shape[0]
            mu_dev = regrouped.shape[1]
            mixed = jnp.dot(metric[0], regrouped.reshape(n_aux, -1), preferred_element_type=jnp.float32)
            mixed = mixed.astype(jnp.bfloat16).reshape(n_aux, mu_dev, NB, occ_c)
            orbital = jnp.transpose(mixed, (1, 2, 0, 3))
            rows = mu_dev * NB
            orbital = orbital.reshape(rows, n_aux * occ_c)
            held = {0: orbital}
            fwd = orbital
            bwd = orbital
            for k in range(1, radius + 1):
                fwd = lax.ppermute(fwd, "grp", shifted(1))
                held[-k] = fwd
                bwd = lax.ppermute(bwd, "grp", shifted(-1))
                held[k] = bwd
            helds.append(held)

        def start_of(off):
            return ring_c[(pos + off) % n] * rows

        def prod(xo, yo):
            out = None
            for held in helds:
                one = jnp.dot(held[xo], held[yo].T, preferred_element_type=jnp.float32)
                out = one if out is None else out + one
            return out

        local = []
        outgoing = {}
        for d in range(n // 2 + 1):
            xo = -((d + 1) // 2)
            yo = xo + d
            blk = prod(xo, yo)
            s = d // 2
            if s == 0:
                local.append((-d, blk))
            else:
                outgoing.setdefault(s, []).append((-d, blk))
            if 0 < d < n // 2:
                outgoing.setdefault(xo, []).append((d, blk.T))
        placed = list(local)
        for s, items in sorted(outgoing.items()):
            stack = jnp.stack([b for _, b in items])
            got = lax.ppermute(stack, "grp", shifted(s))
            placed += [(off, got[i]) for i, (off, _) in enumerate(items)]
        term = jnp.zeros((n * rows, rows), jnp.float32)
        for off, blk in placed:
            term = lax.dynamic_update_slice_in_dim(term, blk, start_of(off), axis=0)
        return scatter_sum(term)

    return body


def solution(mesh):
    return jax.shard_map(
        make_body(ring_order(mesh)),
        mesh=mesh,
        in_specs=(P("rep", "grp", None, None, None), P("rep", None, None), P(), P(), P(), P()),
        out_specs=P("rep", "grp"),
        check_vma=False,
    )
```

```python
import jax
import jax.numpy as jnp
import numpy as np
from jax import lax
from jax.sharding import PartitionSpec as P

NB = 64


def snake(a_size, b_size):
    if a_size % 2:
        return [(a, b) for b, a in snake(b_size, a_size)]
    if b_size == 1:
        return [(a, 0) for a in range(a_size)]
    path = []
    for a in range(a_size):
        cols = range(b_size) if a == 0 else (range(1, b_size) if a % 2 == 0 else range(b_size - 1, 0, -1))
        path += [(a, b) for b in cols]
    path += [(a, 0) for a in range(a_size - 1, 0, -1)]
    return path


def ring_order(mesh):
    n = mesh.shape["grp"]
    try:
        devs = np.asarray(mesh.devices).reshape(n, -1)[:, 0]
        coords = [tuple(d.coords) for d in devs]
    except (AttributeError, TypeError):
        return list(range(n))
    varying = [i for i in range(len(coords[0])) if len({c[i] for c in coords}) > 1]
    if len(varying) == 1:
        key = sorted(range(n), key=lambda g: coords[g][varying[0]])
        return key
    if len(varying) != 2:
        return list(range(n))
    i, j = varying
    avals = sorted({c[i] for c in coords})
    bvals = sorted({c[j] for c in coords})
    where = {(avals.index(c[i]), bvals.index(c[j])): g for g, c in enumerate(coords)}
    if len(where) != n:
        return list(range(n))
    return [where[p] for p in snake(len(avals), len(bvals))]


def scatter_sum(term):
    n_rep = lax.axis_size("rep")
    if n_rep & (n_rep - 1):
        return lax.psum_scatter(term, "rep", scatter_dimension=0, tiled=True)
    me = lax.axis_index("rep")
    bits = n_rep.bit_length() - 1
    per = term.shape[0] // n_rep
    buf = term.reshape((2,) * bits + (per,) + term.shape[1:])
    for b in range(bits):
        d = 1 << b
        axis = buf.ndim - 3
        mine = (me // d) % 2
        keep = lax.dynamic_index_in_dim(buf, mine, axis=axis, keepdims=False)
        send = lax.dynamic_index_in_dim(buf, 1 - mine, axis=axis, keepdims=False)
        got = lax.ppermute(send, "rep", [(i, i ^ d) for i in range(n_rep)])
        buf = keep + got
    return buf.reshape(per, term.shape[1])


def make_body(ring):
    n = len(ring)
    pos_of = np.zeros(n, np.int32)
    for p, g in enumerate(ring):
        pos_of[g] = p
    ring_arr = np.asarray(ring, np.int32)

    def shifted(s):
        return [(ring[p], ring[(p + s) % n]) for p in range(n)]

    def body(three_center, metric, occupied, nu_list, nu_count, block_size):
        n_mu, knu = nu_list.shape
        n_occ = occupied.shape[1]
        aux_dev = three_center.shape[1]
        lanes = jnp.arange(NB, dtype=jnp.int32)
        row_live = lanes[None, :] < block_size[:, None]
        col_live = lanes[None, None, :] < block_size[nu_list][:, :, None]
        slot_live = jnp.arange(knu, dtype=jnp.int32)[None, :] < nu_count[:, None]
        keep = col_live & slot_live[:, :, None]
        picked = occupied.reshape(n_mu, NB, n_occ)[nu_list]
        picked = jnp.where(keep[..., None], picked, jnp.zeros((), jnp.bfloat16))
        pair = 2
        blank = jnp.zeros_like(picked)
        weight = jnp.concatenate(
            [jnp.concatenate([picked, blank], axis=-1), jnp.concatenate([blank, picked], axis=-1)], axis=-2
        )
        tiles = NB // pair
        tc = jnp.swapaxes(three_center[0], 1, 2).reshape(aux_dev, knu, n_mu, tiles, pair * NB)
        half = jnp.einsum("qkmtl,mklc->qmtc", tc, weight, preferred_element_type=jnp.float32)
        half = half.reshape(aux_dev, n_mu, NB, n_occ)
        half = jnp.where(row_live[None, :, :, None], half, 0.0).astype(jnp.bfloat16)
        mu_dev = n_mu // n
        n_split = 2 if mu_dev % 2 == 0 else 1
        mu_c = mu_dev // n_split
        half = half.reshape(aux_dev, n, mu_dev, NB * n_occ)
        me = lax.axis_index("grp")
        pos = jnp.asarray(pos_of)[me]
        ring_c = jnp.asarray(ring_arr)
        radius = n // 4
        helds = []
        for h in range(n_split):
            part = half[:, :, h * mu_c:(h + 1) * mu_c].reshape(aux_dev, n * mu_c, NB * n_occ)
            regrouped = lax.all_to_all(part, "grp", split_axis=1, concat_axis=0, tiled=True)
            n_aux = regrouped.shape[0]
            mixed = jnp.dot(metric[0], regrouped.reshape(n_aux, -1), preferred_element_type=jnp.float32)
            mixed = mixed.astype(jnp.bfloat16).reshape(n_aux, mu_c, NB, n_occ)
            orbital = jnp.transpose(mixed, (1, 2, 0, 3)).reshape(mu_c * NB, n_aux * n_occ)
            held = {0: orbital}
            fwd = orbital
            bwd = orbital
            for k in range(1, radius + 1):
                fwd = lax.ppermute(fwd, "grp", shifted(1))
                held[-k] = fwd
                bwd = lax.ppermute(bwd, "grp", shifted(-1))
                held[k] = bwd
            helds.append(held)
        held = {off: jnp.concatenate([hd[off] for hd in helds], axis=0) for off in helds[0]}
        rows = mu_dev * NB

        def start_of(off):
            return ring_c[(pos + off) % n] * rows

        def prod(xo, yo):
            return jnp.dot(held[xo], held[yo].T, preferred_element_type=jnp.float32)

        local = []
        outgoing = {}
        for d in range(n // 2 + 1):
            xo = -((d + 1) // 2)
            yo = xo + d
            blk = prod(xo, yo)
            s = d // 2
            if s == 0:
                local.append((-d, blk))
            else:
                outgoing.setdefault(s, []).append((-d, blk))
            if 0 < d < n // 2:
                outgoing.setdefault(xo, []).append((d, blk.T))
        placed = list(local)
        for s, items in sorted(outgoing.items()):
            stack = jnp.stack([b for _, b in items])
            got = lax.ppermute(stack, "grp", shifted(s))
            placed += [(off, got[i]) for i, (off, _) in enumerate(items)]
        term = jnp.zeros((n * rows, rows), jnp.float32)
        for off, blk in placed:
            term = lax.dynamic_update_slice_in_dim(term, blk, start_of(off), axis=0)
        return scatter_sum(term)

    return body


def solution(mesh):
    return jax.shard_map(
        make_body(ring_order(mesh)),
        mesh=mesh,
        in_specs=(P("rep", "grp", None, None, None), P("rep", None, None), P(), P(), P(), P()),
        out_specs=P("rep", "grp"),
        check_vma=False,
    )
```

```python
import jax
import jax.numpy as jnp
import numpy as np
from jax import lax
from jax.sharding import PartitionSpec as P

NB = 64


def snake(a_size, b_size):
    if a_size % 2:
        return [(a, b) for b, a in snake(b_size, a_size)]
    if b_size == 1:
        return [(a, 0) for a in range(a_size)]
    path = []
    for a in range(a_size):
        cols = range(b_size) if a == 0 else (range(1, b_size) if a % 2 == 0 else range(b_size - 1, 0, -1))
        path += [(a, b) for b in cols]
    path += [(a, 0) for a in range(a_size - 1, 0, -1)]
    return path


def ring_order(mesh):
    n = mesh.shape["grp"]
    try:
        devs = np.asarray(mesh.devices).reshape(n, -1)[:, 0]
        coords = [tuple(d.coords) for d in devs]
    except (AttributeError, TypeError):
        return list(range(n))
    varying = [i for i in range(len(coords[0])) if len({c[i] for c in coords}) > 1]
    if len(varying) == 1:
        key = sorted(range(n), key=lambda g: coords[g][varying[0]])
        return key
    if len(varying) != 2:
        return list(range(n))
    i, j = varying
    avals = sorted({c[i] for c in coords})
    bvals = sorted({c[j] for c in coords})
    where = {(avals.index(c[i]), bvals.index(c[j])): g for g, c in enumerate(coords)}
    if len(where) != n:
        return list(range(n))
    return [where[p] for p in snake(len(avals), len(bvals))]


def scatter_sum(term):
    n_rep = lax.axis_size("rep")
    if n_rep & (n_rep - 1):
        return lax.psum_scatter(term, "rep", scatter_dimension=0, tiled=True)
    me = lax.axis_index("rep")
    bits = n_rep.bit_length() - 1
    per = term.shape[0] // n_rep
    buf = term.reshape((2,) * bits + (per,) + term.shape[1:])
    for b in range(bits):
        d = 1 << b
        axis = buf.ndim - 3
        mine = (me // d) % 2
        keep = lax.dynamic_index_in_dim(buf, mine, axis=axis, keepdims=False)
        send = lax.dynamic_index_in_dim(buf, 1 - mine, axis=axis, keepdims=False)
        got = lax.ppermute(send, "rep", [(i, i ^ d) for i in range(n_rep)])
        buf = keep + got
    return buf.reshape(per, term.shape[1])


def make_body(ring):
    n = len(ring)
    pos_of = np.zeros(n, np.int32)
    for p, g in enumerate(ring):
        pos_of[g] = p
    ring_arr = np.asarray(ring, np.int32)

    def shifted(s):
        return [(ring[p], ring[(p + s) % n]) for p in range(n)]

    def body(three_center, metric, occupied, nu_list, nu_count, block_size):
        n_mu, knu = nu_list.shape
        n_occ = occupied.shape[1]
        aux_dev = three_center.shape[1]
        lanes = jnp.arange(NB, dtype=jnp.int32)
        row_live = lanes[None, :] < block_size[:, None]
        col_live = lanes[None, None, :] < block_size[nu_list][:, :, None]
        slot_live = jnp.arange(knu, dtype=jnp.int32)[None, :] < nu_count[:, None]
        keep = col_live & slot_live[:, :, None]
        picked = occupied.reshape(n_mu, NB, n_occ)[nu_list]
        picked = jnp.where(keep[..., None], picked, jnp.zeros((), jnp.bfloat16))
        pair = 2
        blank = jnp.zeros_like(picked)
        weight = jnp.concatenate(
            [jnp.concatenate([picked, blank], axis=-1), jnp.concatenate([blank, picked], axis=-1)], axis=-2
        )
        tiles = NB // pair
        tc = jnp.swapaxes(three_center[0], 1, 2).reshape(aux_dev, knu, n_mu, tiles, pair * NB)
        half = jnp.einsum("qkmtl,mklc->qmtc", tc, weight, preferred_element_type=jnp.float32)
        half = half.reshape(aux_dev, n_mu, NB, n_occ)
        half = jnp.where(row_live[None, :, :, None], half, 0.0).astype(jnp.bfloat16)
        mu_dev = n_mu // n
        n_split = mu_dev
        mu_c = mu_dev // n_split
        half = half.reshape(aux_dev, n, mu_dev, NB * n_occ)
        me = lax.axis_index("grp")
        pos = jnp.asarray(pos_of)[me]
        ring_c = jnp.asarray(ring_arr)
        radius = n // 4
        helds = []
        for h in range(n_split):
            part = half[:, :, h * mu_c:(h + 1) * mu_c].reshape(aux_dev, n * mu_c, NB * n_occ)
            regrouped = lax.all_to_all(part, "grp", split_axis=1, concat_axis=0, tiled=True)
            n_aux = regrouped.shape[0]
            mixed = jnp.dot(metric[0], regrouped.reshape(n_aux, -1), preferred_element_type=jnp.float32)
            mixed = mixed.astype(jnp.bfloat16).reshape(n_aux, mu_c, NB, n_occ)
            orbital = jnp.transpose(mixed, (1, 2, 0, 3)).reshape(mu_c * NB, n_aux * n_occ)
            held = {0: orbital}
            fwd = orbital
            bwd = orbital
            for k in range(1, radius + 1):
                fwd = lax.ppermute(fwd, "grp", shifted(1))
                held[-k] = fwd
                bwd = lax.ppermute(bwd, "grp", shifted(-1))
                held[k] = bwd
            helds.append(held)
        held = {off: jnp.concatenate([hd[off] for hd in helds], axis=0) for off in helds[0]}
        rows = mu_dev * NB

        def start_of(off):
            return ring_c[(pos + off) % n] * rows

        def prod(xo, yo):
            return jnp.dot(held[xo], held[yo].T, preferred_element_type=jnp.float32)

        local = []
        outgoing = {}
        for d in range(n // 2 + 1):
            xo = -((d + 1) // 2)
            yo = xo + d
            blk = prod(xo, yo)
            s = d // 2
            if s == 0:
                local.append((-d, blk))
            else:
                outgoing.setdefault(s, []).append((-d, blk))
            if 0 < d < n // 2:
                outgoing.setdefault(xo, []).append((d, blk.T))
        placed = list(local)
        for s, items in sorted(outgoing.items()):
            stack = jnp.stack([b for _, b in items])
            got = lax.ppermute(stack, "grp", shifted(s))
            placed += [(off, got[i]) for i, (off, _) in enumerate(items)]
        term = jnp.zeros((n * rows, rows), jnp.float32)
        for off, blk in placed:
            term = lax.dynamic_update_slice_in_dim(term, blk, start_of(off), axis=0)
        return scatter_sum(term)

    return body


def solution(mesh):
    return jax.shard_map(
        make_body(ring_order(mesh)),
        mesh=mesh,
        in_specs=(P("rep", "grp", None, None, None), P("rep", None, None), P(), P(), P(), P()),
        out_specs=P("rep", "grp"),
        check_vma=False,
    )
```

```python
import jax
import jax.numpy as jnp
import numpy as np
from jax import lax
from jax.sharding import PartitionSpec as P

NB = 64


def snake(a_size, b_size):
    if a_size % 2:
        return [(a, b) for b, a in snake(b_size, a_size)]
    if b_size == 1:
        return [(a, 0) for a in range(a_size)]
    path = []
    for a in range(a_size):
        cols = range(b_size) if a == 0 else (range(1, b_size) if a % 2 == 0 else range(b_size - 1, 0, -1))
        path += [(a, b) for b in cols]
    path += [(a, 0) for a in range(a_size - 1, 0, -1)]
    return path


def ring_order(mesh):
    n = mesh.shape["grp"]
    try:
        devs = np.asarray(mesh.devices).reshape(n, -1)[:, 0]
        coords = [tuple(d.coords) for d in devs]
    except (AttributeError, TypeError):
        return list(range(n))
    varying = [i for i in range(len(coords[0])) if len({c[i] for c in coords}) > 1]
    if len(varying) == 1:
        key = sorted(range(n), key=lambda g: coords[g][varying[0]])
        return key
    if len(varying) != 2:
        return list(range(n))
    i, j = varying
    avals = sorted({c[i] for c in coords})
    bvals = sorted({c[j] for c in coords})
    where = {(avals.index(c[i]), bvals.index(c[j])): g for g, c in enumerate(coords)}
    if len(where) != n:
        return list(range(n))
    return [where[p] for p in snake(len(avals), len(bvals))]


def scatter_sum(term):
    n_rep = lax.axis_size("rep")
    if n_rep & (n_rep - 1):
        return lax.psum_scatter(term, "rep", scatter_dimension=0, tiled=True)
    me = lax.axis_index("rep")
    bits = n_rep.bit_length() - 1
    per = term.shape[0] // n_rep
    buf = term.reshape((2,) * bits + (per,) + term.shape[1:])
    for b in range(bits):
        d = 1 << b
        axis = buf.ndim - 3
        mine = (me // d) % 2
        keep = lax.dynamic_index_in_dim(buf, mine, axis=axis, keepdims=False)
        send = lax.dynamic_index_in_dim(buf, 1 - mine, axis=axis, keepdims=False)
        got = lax.ppermute(send, "rep", [(i, i ^ d) for i in range(n_rep)])
        buf = keep + got
    return buf.reshape(per, term.shape[1])


def make_body(ring):
    n = len(ring)
    pos_of = np.zeros(n, np.int32)
    for p, g in enumerate(ring):
        pos_of[g] = p
    ring_arr = np.asarray(ring, np.int32)

    def shifted(s):
        return [(ring[p], ring[(p + s) % n]) for p in range(n)]

    def body(three_center, metric, occupied, nu_list, nu_count, block_size):
        n_mu, knu = nu_list.shape
        n_occ = occupied.shape[1]
        aux_dev = three_center.shape[1]
        lanes = jnp.arange(NB, dtype=jnp.int32)
        row_live = lanes[None, :] < block_size[:, None]
        col_live = lanes[None, None, :] < block_size[nu_list][:, :, None]
        slot_live = jnp.arange(knu, dtype=jnp.int32)[None, :] < nu_count[:, None]
        keep = col_live & slot_live[:, :, None]
        picked = occupied.reshape(n_mu, NB, n_occ)[nu_list]
        picked = jnp.where(keep[..., None], picked, jnp.zeros((), jnp.bfloat16))
        pair = 2
        blank = jnp.zeros_like(picked)
        weight = jnp.concatenate(
            [jnp.concatenate([picked, blank], axis=-1), jnp.concatenate([blank, picked], axis=-1)], axis=-2
        )
        tiles = NB // pair
        tc = jnp.swapaxes(three_center[0], 1, 2).reshape(aux_dev, knu, n_mu, tiles, pair * NB)
        mu_dev = n_mu // n
        n_split = 2 if mu_dev % 2 == 0 else 1
        mu_c = mu_dev // n_split
        me = lax.axis_index("grp")
        pos = jnp.asarray(pos_of)[me]
        ring_c = jnp.asarray(ring_arr)
        radius = n // 4
        tc6 = tc.reshape(aux_dev, knu, n, mu_dev, tiles, pair * NB)
        w5 = weight.reshape((n, mu_dev) + weight.shape[1:])
        live3 = row_live.reshape(n, mu_dev, NB)
        helds = []
        for h in range(n_split):
            sl = slice(h * mu_c, (h + 1) * mu_c)
            tc_h = tc6[:, :, :, sl].reshape(aux_dev, knu, n * mu_c, tiles, pair * NB)
            w_h = w5[:, sl].reshape((n * mu_c,) + weight.shape[1:])
            live_h = live3[:, sl].reshape(n * mu_c, NB)
            part = jnp.einsum("qkmtl,mklc->qmtc", tc_h, w_h, preferred_element_type=jnp.float32)
            part = part.reshape(aux_dev, n * mu_c, NB, n_occ)
            part = jnp.where(live_h[None, :, :, None], part, 0.0).astype(jnp.bfloat16)
            part = part.reshape(aux_dev, n * mu_c, NB * n_occ)
            regrouped = lax.all_to_all(part, "grp", split_axis=1, concat_axis=0, tiled=True)
            n_aux = regrouped.shape[0]
            mixed = jnp.dot(metric[0], regrouped.reshape(n_aux, -1), preferred_element_type=jnp.float32)
            mixed = mixed.astype(jnp.bfloat16).reshape(n_aux, mu_c, NB, n_occ)
            orbital = jnp.transpose(mixed, (1, 2, 0, 3)).reshape(mu_c * NB, n_aux * n_occ)
            held = {0: orbital}
            fwd = orbital
            bwd = orbital
            for k in range(1, radius + 1):
                fwd = lax.ppermute(fwd, "grp", shifted(1))
                held[-k] = fwd
                bwd = lax.ppermute(bwd, "grp", shifted(-1))
                held[k] = bwd
            helds.append(held)
        held = {off: jnp.concatenate([hd[off] for hd in helds], axis=0) for off in helds[0]}
        rows = mu_dev * NB

        def start_of(off):
            return ring_c[(pos + off) % n] * rows

        def prod(xo, yo):
            return jnp.dot(held[xo], held[yo].T, preferred_element_type=jnp.float32)

        local = []
        outgoing = {}
        for d in range(n // 2 + 1):
            xo = -((d + 1) // 2)
            yo = xo + d
            blk = prod(xo, yo)
            s = d // 2
            if s == 0:
                local.append((-d, blk))
            else:
                outgoing.setdefault(s, []).append((-d, blk))
            if 0 < d < n // 2:
                outgoing.setdefault(xo, []).append((d, blk.T))
        placed = list(local)
        for s, items in sorted(outgoing.items()):
            stack = jnp.stack([b for _, b in items])
            got = lax.ppermute(stack, "grp", shifted(s))
            placed += [(off, got[i]) for i, (off, _) in enumerate(items)]
        term = jnp.zeros((n * rows, rows), jnp.float32)
        for off, blk in placed:
            term = lax.dynamic_update_slice_in_dim(term, blk, start_of(off), axis=0)
        return scatter_sum(term)

    return body


def solution(mesh):
    return jax.shard_map(
        make_body(ring_order(mesh)),
        mesh=mesh,
        in_specs=(P("rep", "grp", None, None, None), P("rep", None, None), P(), P(), P(), P()),
        out_specs=P("rep", "grp"),
        check_vma=False,
    )
```

```python
import jax
import jax.numpy as jnp
import numpy as np
from jax import lax
from jax.sharding import PartitionSpec as P

NB = 64


def snake(a_size, b_size):
    if a_size % 2:
        return [(a, b) for b, a in snake(b_size, a_size)]
    if b_size == 1:
        return [(a, 0) for a in range(a_size)]
    path = []
    for a in range(a_size):
        cols = range(b_size) if a == 0 else (range(1, b_size) if a % 2 == 0 else range(b_size - 1, 0, -1))
        path += [(a, b) for b in cols]
    path += [(a, 0) for a in range(a_size - 1, 0, -1)]
    return path


def ring_order(mesh):
    n = mesh.shape["grp"]
    try:
        devs = np.asarray(mesh.devices).reshape(n, -1)[:, 0]
        coords = [tuple(d.coords) for d in devs]
    except (AttributeError, TypeError):
        return list(range(n))
    varying = [i for i in range(len(coords[0])) if len({c[i] for c in coords}) > 1]
    if len(varying) == 1:
        key = sorted(range(n), key=lambda g: coords[g][varying[0]])
        return key
    if len(varying) != 2:
        return list(range(n))
    i, j = varying
    avals = sorted({c[i] for c in coords})
    bvals = sorted({c[j] for c in coords})
    where = {(avals.index(c[i]), bvals.index(c[j])): g for g, c in enumerate(coords)}
    if len(where) != n:
        return list(range(n))
    return [where[p] for p in snake(len(avals), len(bvals))]


def scatter_sum(term):
    n_rep = lax.axis_size("rep")
    if n_rep & (n_rep - 1):
        return lax.psum_scatter(term, "rep", scatter_dimension=0, tiled=True)
    me = lax.axis_index("rep")
    bits = n_rep.bit_length() - 1
    per = term.shape[0] // n_rep
    buf = term.reshape((2,) * bits + (per,) + term.shape[1:])
    for b in range(bits):
        d = 1 << b
        axis = buf.ndim - 3
        mine = (me // d) % 2
        keep = lax.dynamic_index_in_dim(buf, mine, axis=axis, keepdims=False)
        send = lax.dynamic_index_in_dim(buf, 1 - mine, axis=axis, keepdims=False)
        got = lax.ppermute(send, "rep", [(i, i ^ d) for i in range(n_rep)])
        buf = keep + got
    return buf.reshape(per, term.shape[1])


def make_body(ring):
    n = len(ring)
    pos_of = np.zeros(n, np.int32)
    for p, g in enumerate(ring):
        pos_of[g] = p
    ring_arr = np.asarray(ring, np.int32)

    def shifted(s):
        return [(ring[p], ring[(p + s) % n]) for p in range(n)]

    def body(three_center, metric, occupied, nu_list, nu_count, block_size):
        n_mu, knu = nu_list.shape
        n_occ = occupied.shape[1]
        aux_dev = three_center.shape[1]
        lanes = jnp.arange(NB, dtype=jnp.int32)
        row_live = lanes[None, :] < block_size[:, None]
        col_live = lanes[None, None, :] < block_size[nu_list][:, :, None]
        slot_live = jnp.arange(knu, dtype=jnp.int32)[None, :] < nu_count[:, None]
        keep = col_live & slot_live[:, :, None]
        picked = occupied.reshape(n_mu, NB, n_occ)[nu_list]
        picked = jnp.where(keep[..., None], picked, jnp.zeros((), jnp.bfloat16))
        pair = 2
        blank = jnp.zeros_like(picked)
        weight = jnp.concatenate(
            [jnp.concatenate([picked, blank], axis=-1), jnp.concatenate([blank, picked], axis=-1)], axis=-2
        )
        tiles = NB // pair
        tc = jnp.swapaxes(three_center[0], 1, 2).reshape(aux_dev, knu, n_mu, tiles, pair * NB)
        half = jnp.einsum("qkmtl,mklc->qmtc", tc, weight, preferred_element_type=jnp.float32)
        half = half.reshape(aux_dev, n_mu, NB, n_occ)
        half = jnp.where(row_live[None, :, :, None], half, 0.0).astype(jnp.bfloat16)
        mu_dev = n_mu // n
        bounds = [0, 1, mu_dev] if mu_dev > 1 else [0, mu_dev]
        half = half.reshape(aux_dev, n, mu_dev, NB * n_occ)
        me = lax.axis_index("grp")
        pos = jnp.asarray(pos_of)[me]
        ring_c = jnp.asarray(ring_arr)
        radius = n // 4
        helds = []
        for lo, hi in zip(bounds[:-1], bounds[1:]):
            mu_c = hi - lo
            part = half[:, :, lo:hi].reshape(aux_dev, n * mu_c, NB * n_occ)
            regrouped = lax.all_to_all(part, "grp", split_axis=1, concat_axis=0, tiled=True)
            n_aux = regrouped.shape[0]
            mixed = jnp.dot(metric[0], regrouped.reshape(n_aux, -1), preferred_element_type=jnp.float32)
            mixed = mixed.astype(jnp.bfloat16).reshape(n_aux, mu_c, NB, n_occ)
            orbital = jnp.transpose(mixed, (1, 2, 0, 3)).reshape(mu_c * NB, n_aux * n_occ)
            held = {0: orbital}
            fwd = orbital
            bwd = orbital
            for k in range(1, radius + 1):
                fwd = lax.ppermute(fwd, "grp", shifted(1))
                held[-k] = fwd
                bwd = lax.ppermute(bwd, "grp", shifted(-1))
                held[k] = bwd
            helds.append(held)
        held = {off: jnp.concatenate([hd[off] for hd in helds], axis=0) for off in helds[0]}
        rows = mu_dev * NB

        def start_of(off):
            return ring_c[(pos + off) % n] * rows

        def prod(xo, yo):
            return jnp.dot(held[xo], held[yo].T, preferred_element_type=jnp.float32)

        local = []
        outgoing = {}
        for d in range(n // 2 + 1):
            xo = -((d + 1) // 2)
            yo = xo + d
            blk = prod(xo, yo)
            s = d // 2
            if s == 0:
                local.append((-d, blk))
            else:
                outgoing.setdefault(s, []).append((-d, blk))
            if 0 < d < n // 2:
                outgoing.setdefault(xo, []).append((d, blk.T))
        placed = list(local)
        for s, items in sorted(outgoing.items()):
            stack = jnp.stack([b for _, b in items])
            got = lax.ppermute(stack, "grp", shifted(s))
            placed += [(off, got[i]) for i, (off, _) in enumerate(items)]
        term = jnp.zeros((n * rows, rows), jnp.float32)
        for off, blk in placed:
            term = lax.dynamic_update_slice_in_dim(term, blk, start_of(off), axis=0)
        return scatter_sum(term)

    return body


def solution(mesh):
    return jax.shard_map(
        make_body(ring_order(mesh)),
        mesh=mesh,
        in_specs=(P("rep", "grp", None, None, None), P("rep", None, None), P(), P(), P(), P()),
        out_specs=P("rep", "grp"),
        check_vma=False,
    )
```
